512 devices in a mesh: ctx: 32 (over x, z_hi, core), head: 16 (over z_lo, y).
Axes of the slice: x: 4, y: 4, z: 16 (z_hi: 4, z_lo: 4; z = z_hi * 4 + z_lo), core: 2. Of those that a mesh axis runs over, the one named last changes fastest.
Arguments:
- queries: bfloat16 [16384, 64, 128], P('ctx', 'head'), may hold values from -18 to 18
- key_rows: bfloat16 [4, 16384, 128], P(None, 'ctx'), may hold values from -18 to 18
- value_rows: bfloat16 [4, 16384, 128], P(None, 'ctx'), may hold values from -6 to 6
- out_grad: bfloat16 [16384, 64, 128], P('ctx', 'head'), may hold values from -36 to 36
- selected: int32 [256, 4, 16], P('ctx'), may hold values from 0 to 255, as said below
- live_slots: int32 [256, 4, 16], P('ctx'), may hold values from 0 to 1, as said below
Outputs:
- query_grad: bfloat16 [16384, 64, 128], P('ctx', 'head')
- key_grad: float32 [4, 16384, 128], P(None, 'ctx')
- value_grad: float32 [4, 16384, 128], P(None, 'ctx')
The draws below stay inside these ranges and needn't reach their ends.
Inputs may be any that keep to these rules, and one draw needn't show every extreme that they name: `selected`: slot 0 of query block b holds b with live_slots 1. Used slots hold distinct blocks x with x <= b and x >= (b // 8 - 6) * 8; used slots come before unused ones, and unused slots hold b. The number of used slots varies between query blocks. `live_slots`: slot 0 is always 1.
All inputs are finite; a program needn't handle non-finite values.
Results may differ from the reference program's by a relative error of at most 0.017.
Values may be sent and summed in bfloat16 or wider, within the bound.
No kernel may reach another device: no remote copies, remote signals or barrier semaphores. Data moves between devices by JAX's collectives and lax.ppermute only.
A program may use at most 64 MiB of HBM per device.

```python
import jax
import jax.numpy as jnp
from jax import lax

DH = 128
HPG = 16
BLOCK = 64
SEL = 16
REACH = 6
HEADS = 64
GROUPS = 4
QB_DEV = 8
TOKENS = 16384
NQB = 256


def draw_queries(key, part):
    result = jax.random.normal(jax.random.fold_in(key, 13), (TOKENS, HEADS, DH), jnp.float32)
    return result.astype(jnp.bfloat16)


def draw_key_rows(key, part):
    result = jax.random.normal(jax.random.fold_in(key, 23), (GROUPS, TOKENS, DH), jnp.float32)
    return result.astype(jnp.bfloat16)


def selection_table(key):
    source = jax.random.fold_in(key, 202)
    farthest = (REACH + 1) * QB_DEV - 1
    distance = jnp.arange(1, farthest + 1, dtype=jnp.int32)
    block_index = jnp.arange(NQB, dtype=jnp.int32)[:, None, None]
    allowed = (distance[None, None, :] <= block_index % QB_DEV + REACH * QB_DEV) & (distance[None, None, :] <= block_index)
    allowed = jnp.broadcast_to(allowed, (NQB, GROUPS, farthest))
    ranking = jax.random.randint(source, (NQB, GROUPS, farthest), 0, 1 << 20, dtype=jnp.int32) * farthest + (distance - 1)[None, None, :]
    ranking = jnp.where(allowed, ranking, ranking + (1 << 20) * farthest)
    order = jnp.argsort(ranking, axis=-1)[:, :, :SEL - 1].astype(jnp.int32)
    usable = jnp.take_along_axis(allowed, order, axis=-1)
    used_count = jax.random.randint(jax.random.fold_in(source, 7), (NQB, GROUPS, 1), SEL // 2, SEL + 1, dtype=jnp.int32)
    slot_pos = jnp.arange(1, SEL, dtype=jnp.int32)[None, None, :]
    usable = usable & (slot_pos < used_count)
    block_full = jnp.broadcast_to(block_index, (NQB, GROUPS, 1))
    chosen = jnp.where(usable, block_full - (order + 1), block_full)
    selected = jnp.concatenate([block_full, chosen], axis=-1).astype(jnp.int32)
    live_mask = jnp.concatenate([jnp.ones((NQB, GROUPS, 1), jnp.int32), usable.astype(jnp.int32)], axis=-1)
    return (selected, live_mask)


def draw_selected(key, part):
    return selection_table(key)[0]


def draw_live_slots(key, part):
    return selection_table(key)[1]


def levels(rng, extent, shards, least, largest):
    gain, own = 1.0, jax.random.fold_in(rng, 6)
    for axis_at, blocks in shards:
        steps = jnp.exp(jax.random.uniform(jax.random.fold_in(own, axis_at), (blocks,), jnp.float32, least / len(shards), largest / len(shards)))
        gain = gain * jnp.repeat(steps, extent[axis_at] // blocks).reshape([-1 if axis == axis_at else 1 for axis in range(len(extent))])
    return gain


def bell_draw(rng, shape, scale, bound, shards=(), kind=jnp.bfloat16):
    values = jax.random.normal(rng, shape, jnp.float32) * scale
    if len(shards) > 0:
        values = levels(rng, shape, shards, -0.22, 0.18) * values
    return jnp.clip(values, min=-bound, max=bound).astype(kind)


def setup_inputs(seed: int = 0) -> dict:
    key_of = jax.random.split(jax.random.key(seed), 7)
    queries = draw_queries(jax.random.fold_in(key_of[6], 71), 0)
    key_rows = draw_key_rows(jax.random.fold_in(key_of[6], 71), 0)
    value_rows = bell_draw(key_of[2], (GROUPS, TOKENS, DH), 1.0, 6.0, ((1, 32),))
    out_grad = bell_draw(key_of[3], (TOKENS, HEADS, DH), 6.0, 36.0, ((0, 32), (1, 16)))
    selected = draw_selected(jax.random.fold_in(key_of[6], 71), 0)
    live_slots = draw_live_slots(jax.random.fold_in(key_of[6], 71), 0)
    return {"queries": queries, "key_rows": key_rows, "value_rows": value_rows, "out_grad": out_grad, "selected": selected, "live_slots": live_slots}


def visible_mask(chosen, live_mask, block_id, width):
    causal = jnp.arange(width)[:, None] >= jnp.arange(width)[None, :]
    earlier = (chosen < block_id)[None, :, None]
    allowed = (live_mask == 1)[None, :, None] & (earlier | causal[:, None, :])
    return allowed.reshape(width, -1)


def block_grads(q_blk, do_blk, k_sel, v_sel, allowed, inv_root):
    scores = jnp.einsum('qhd,nd->hqn', q_blk, k_sel) * inv_root
    scores = jnp.where(allowed[None], scores, -1e30)
    row_max = jnp.max(scores, axis=-1, keepdims=True)
    shifted = jnp.exp(scores - row_max)
    weights = shifted / jnp.sum(shifted, axis=-1, keepdims=True)
    weights_b = lax.optimization_barrier(weights.astype(jnp.bfloat16)).astype(jnp.float32)
    output = jnp.einsum('hqn,nd->qhd', weights_b, v_sel)
    row_delta = jnp.sum(do_blk * output, axis=-1)
    prob_grad = jnp.einsum('qhd,nd->hqn', do_blk, v_sel)
    score_grad = weights * (prob_grad - jnp.transpose(row_delta)[:, :, None])
    score_b = lax.optimization_barrier(score_grad.astype(jnp.bfloat16)).astype(jnp.float32)
    query_part = jnp.einsum('hqn,nd->qhd', score_b, k_sel) * inv_root
    key_part = jnp.einsum('hqn,qhd->nd', score_b, q_blk) * inv_root
    value_part = jnp.einsum('hqn,qhd->nd', weights_b, do_blk)
    return query_part, key_part, value_part


def reference(queries, key_rows, value_rows, out_grad, selected, live_slots):
    groups = key_rows.shape[0]
    total = queries.shape[0]
    nblocks = total // BLOCK
    inv_root = DH ** -0.5
    q_all = queries.astype(jnp.float32).reshape(nblocks, BLOCK, groups, HPG, DH)
    do_all = out_grad.astype(jnp.float32).reshape(nblocks, BLOCK, groups, HPG, DH)
    k_all = key_rows.astype(jnp.float32).reshape(groups, nblocks, BLOCK, DH)
    v_all = value_rows.astype(jnp.float32).reshape(groups, nblocks, BLOCK, DH)
    group_ids = jnp.arange(groups, dtype=jnp.int32)

    def advance(running, block_id):
        key_acc, value_acc = running
        chosen = selected[block_id].astype(jnp.int32)
        live_mask = live_slots[block_id]
        k_sel = k_all[group_ids[:, None], chosen].reshape(groups, SEL * BLOCK, DH)
        v_sel = v_all[group_ids[:, None], chosen].reshape(groups, SEL * BLOCK, DH)
        q_blk = jnp.transpose(q_all[block_id], (1, 0, 2, 3))
        do_blk = jnp.transpose(do_all[block_id], (1, 0, 2, 3))
        allowed = jax.vmap(visible_mask, in_axes=(0, 0, None, None))(chosen, live_mask, block_id, BLOCK)
        query_part, key_part, value_part = jax.vmap(block_grads, in_axes=(0, 0, 0, 0, 0, None))(
            q_blk, do_blk, k_sel, v_sel, allowed, inv_root)
        key_acc = key_acc.at[group_ids[:, None], chosen].add(key_part.reshape(groups, SEL, BLOCK, DH))
        value_acc = value_acc.at[group_ids[:, None], chosen].add(value_part.reshape(groups, SEL, BLOCK, DH))
        return (key_acc, value_acc), jnp.transpose(query_part, (1, 0, 2, 3))

    zeros = jnp.zeros((groups, nblocks, BLOCK, DH), jnp.float32)
    (key_acc, value_acc), query_parts = lax.scan(advance, (zeros, zeros), jnp.arange(nblocks, dtype=jnp.int32))
    query_grad = query_parts.reshape(total, groups * HPG, DH).astype(jnp.bfloat16)
    return query_grad, key_acc.reshape(groups, total, DH), value_acc.reshape(groups, total, DH)
```

```python
import jax
import jax.numpy as jnp
import numpy as np
from jax import lax
from jax.sharding import Mesh
from jax.sharding import PartitionSpec as P

HPG = 16
BLOCK = 64
REACH = 6


def shifted_2(value, axis, steps):
    count = lax.axis_size(axis)
    leading, last = (max(0, -steps), min(count, count - steps))
    return lax.ppermute(value, axis, [(source, source + steps) for source in range(leading, last)])


def visible_mask(chosen, live_mask, block_id, width):
    causal = jnp.arange(width)[:, None] >= jnp.arange(width)[None, :]
    earlier = (chosen < block_id)[None, :, None]
    allowed = (live_mask == 1)[None, :, None] & (earlier | causal[:, None, :])
    return allowed.reshape(width, -1)


def tile_grads(q_pair, do_pair, k_sel, v_sel, allowed, inv_root):
    scores = (
        jnp.einsum("bqhd,bnd->bhqn", q_pair, k_sel, preferred_element_type=jnp.float32) * inv_root
    )
    scores = jnp.where(allowed[:, None], scores, -1e30)
    row_max = jnp.max(scores, axis=-1, keepdims=True)
    shifted = jnp.exp(scores - row_max)
    weights = shifted / jnp.sum(shifted, axis=-1, keepdims=True)
    weights_b = weights.astype(jnp.bfloat16)
    output = jnp.einsum("bhqn,bnd->bqhd", weights_b, v_sel, preferred_element_type=jnp.float32)
    row_delta = jnp.sum(do_pair.astype(jnp.float32) * output, axis=-1)
    prob_grad = jnp.einsum("bqhd,bnd->bhqn", do_pair, v_sel, preferred_element_type=jnp.float32)
    score_grad = weights * (prob_grad - jnp.transpose(row_delta, (0, 2, 1))[..., None])
    score_b = score_grad.astype(jnp.bfloat16)
    query_part = (
        jnp.einsum("bhqn,bnd->bqhd", score_b, k_sel, preferred_element_type=jnp.float32) * inv_root
    )
    key_part = (
        jnp.einsum("bhqn,bqhd->bnd", score_b, q_pair, preferred_element_type=jnp.float32) * inv_root
    )
    value_part = jnp.einsum(
        "bhqn,bqhd->bnd", weights_b, do_pair, preferred_element_type=jnp.float32
    )
    return (query_part.astype(jnp.bfloat16), key_part, value_part)


def per_device(queries, key_rows, value_rows, out_grad, selected, live_slots):
    tokens_here, heads_here, width = queries.shape
    groups = key_rows.shape[0]
    blocks_here = tokens_here // BLOCK
    reach_span = REACH + 1
    inv_root = width ** (-0.5)
    ctx_index = lax.axis_index("ctx")
    group_index = lax.axis_index("grp")
    part_index = lax.axis_index("sub")
    parts_count = lax.axis_size("sub")
    quarter = tokens_here // parts_count
    own_tiles = jnp.stack(
        [
            lax.dynamic_index_in_dim(key_rows, group_index, 0, keepdims=False),
            lax.dynamic_index_in_dim(value_rows, group_index, 0, keepdims=False),
        ]
    )
    own_part = lax.dynamic_slice_in_dim(own_tiles, part_index * quarter, quarter, axis=1)
    fetched = []
    moving = own_part
    for offset in range(REACH):
        moving = shifted_2(moving, "ctx", 1)
        fetched.append(moving)
    gathered = lax.all_gather(jnp.stack(fetched), "sub", axis=2, tiled=True)
    tile_store = jnp.concatenate([own_tiles[None], gathered], axis=0)
    key_tiles = tile_store[:, 0].reshape(reach_span * blocks_here, BLOCK, width)
    value_tiles = tile_store[:, 1].reshape(reach_span * blocks_here, BLOCK, width)
    chosen = lax.dynamic_index_in_dim(selected, group_index, 1, keepdims=False)
    live_mask = lax.dynamic_index_in_dim(live_slots, group_index, 1, keepdims=False)
    block_ids = ctx_index * blocks_here + jnp.arange(blocks_here, dtype=jnp.int32)
    slot_index = (ctx_index - chosen // blocks_here) * blocks_here + chosen % blocks_here
    pair_count = blocks_here // 2

    def accumulate(running, inputs):
        q_pair, do_pair, slot_pair, chosen_pair, live_pair, block_pair = inputs
        k_sel = key_tiles[slot_pair].reshape(2, -1, width)
        v_sel = value_tiles[slot_pair].reshape(2, -1, width)
        allowed = jax.vmap(visible_mask, in_axes=(0, 0, 0, None))(
            chosen_pair, live_pair, block_pair, BLOCK
        )
        query_part, key_part, value_part = tile_grads(
            q_pair, do_pair, k_sel, v_sel, allowed, inv_root
        )
        stacked = jnp.stack([key_part, value_part]).reshape(2, -1, BLOCK, width)
        running = running.at[:, slot_pair.reshape(-1)].add(stacked)
        return (running, query_part)

    initial = jnp.zeros((2, reach_span * blocks_here, BLOCK, width), jnp.float32)
    inputs = (
        queries.reshape(pair_count, 2, BLOCK, heads_here, width),
        out_grad.reshape(pair_count, 2, BLOCK, heads_here, width),
        slot_index.reshape(pair_count, 2, -1),
        chosen.reshape(pair_count, 2, -1),
        live_mask.reshape(pair_count, 2, -1),
        block_ids.reshape(pair_count, 2),
    )
    grads, query_parts = lax.scan(accumulate, initial, inputs)
    grads = grads.reshape(2, reach_span, tokens_here, width)
    parts = lax.psum_scatter(
        grads.astype(jnp.bfloat16), "sub", scatter_dimension=2, tiled=True
    ).astype(jnp.float32)
    running = parts[:, REACH]
    for offset in range(REACH - 1, -1, -1):
        running = (
            shifted_2(running.astype(jnp.bfloat16), "ctx", -1).astype(running.dtype)
            + parts[:, offset]
        )
    summed = lax.all_gather(running.astype(jnp.bfloat16), ("grp", "sub"), axis=1, tiled=True)
    summed = summed.astype(jnp.float32).reshape(2, groups, tokens_here, width)
    query_grad = query_parts.reshape(tokens_here, heads_here, width)
    return (query_grad, summed[0], summed[1])


def solution(mesh):
    ctx_count, head_count = mesh.devices.shape
    groups = 4
    split = Mesh(
        np.asarray(mesh.devices).reshape(ctx_count, groups, head_count // groups),
        ("ctx", "grp", "sub"),
    )
    heads = ("grp", "sub")
    return jax.shard_map(
        per_device,
        mesh=split,
        in_specs=(
            P("ctx", heads, None),
            P(None, "ctx", None),
            P(None, "ctx", None),
            P("ctx", heads, None),
            P("ctx", None, None),
            P("ctx", None, None),
        ),
        out_specs=(P("ctx", heads, None), P(None, "ctx", None), P(None, "ctx", None)),
        check_vma=False,
    )
```

```python
import jax
import jax.numpy as jnp
import numpy as np
from jax import lax
from jax.sharding import Mesh
from jax.sharding import PartitionSpec as P

HPG = 16
BLOCK = 64
REACH = 6


def shifted_2(value, axis, steps):
    count = lax.axis_size(axis)
    leading, last = (max(0, -steps), min(count, count - steps))
    return lax.ppermute(value, axis, [(source, source + steps) for source in range(leading, last)])


def cycled(value, axis, steps):
    count = lax.axis_size(axis)
    return lax.ppermute(value, axis, [(source, (source + steps) % count) for source in range(count)])


def visible_mask(chosen, live_mask, block_id, width):
    causal = jnp.arange(width)[:, None] >= jnp.arange(width)[None, :]
    earlier = (chosen < block_id)[None, :, None]
    allowed = (live_mask == 1)[None, :, None] & (earlier | causal[:, None, :])
    return allowed.reshape(width, -1)


def tile_grads(q_pair, do_pair, k_sel, v_sel, allowed, inv_root):
    scores = (
        jnp.einsum("bqhd,bnd->bhqn", q_pair, k_sel, preferred_element_type=jnp.float32) * inv_root
    )
    scores = jnp.where(allowed[:, None], scores, -1e30)
    row_max = jnp.max(scores, axis=-1, keepdims=True)
    shifted = jnp.exp(scores - row_max)
    weights = shifted / jnp.sum(shifted, axis=-1, keepdims=True)
    weights_b = weights.astype(jnp.bfloat16)
    output = jnp.einsum("bhqn,bnd->bqhd", weights_b, v_sel, preferred_element_type=jnp.float32)
    row_delta = jnp.sum(do_pair.astype(jnp.float32) * output, axis=-1)
    prob_grad = jnp.einsum("bqhd,bnd->bhqn", do_pair, v_sel, preferred_element_type=jnp.float32)
    score_grad = weights * (prob_grad - jnp.transpose(row_delta, (0, 2, 1))[..., None])
    score_b = score_grad.astype(jnp.bfloat16)
    query_part = (
        jnp.einsum("bhqn,bnd->bqhd", score_b, k_sel, preferred_element_type=jnp.float32) * inv_root
    )
    key_part = (
        jnp.einsum("bhqn,bqhd->bnd", score_b, q_pair, preferred_element_type=jnp.float32) * inv_root
    )
    value_part = jnp.einsum(
        "bhqn,bqhd->bnd", weights_b, do_pair, preferred_element_type=jnp.float32
    )
    return (query_part.astype(jnp.bfloat16), key_part, value_part)


def per_device(queries, key_rows, value_rows, out_grad, selected, live_slots):
    tokens_here, heads_here, width = queries.shape
    groups = key_rows.shape[0]
    blocks_here = tokens_here // BLOCK
    reach_span = REACH + 1
    inv_root = width ** (-0.5)
    ctx_index = lax.axis_index("ctx")
    group_index = lax.axis_index("grp")
    part_index = lax.axis_index("sub")
    parts_count = lax.axis_size("sub")
    quarter = tokens_here // parts_count
    own_tiles = jnp.stack(
        [
            lax.dynamic_index_in_dim(key_rows, group_index, 0, keepdims=False),
            lax.dynamic_index_in_dim(value_rows, group_index, 0, keepdims=False),
        ]
    )
    rolled = jnp.roll(own_tiles, -part_index * quarter, axis=1)
    own_part = rolled[:, :quarter]
    fetched = jnp.stack([shifted_2(own_part, "ctx", offset) for offset in range(1, reach_span)])
    pieces = [fetched] + [cycled(fetched, "sub", -step) for step in range(1, parts_count)]
    tile_store = jnp.concatenate([rolled[None], jnp.concatenate(pieces, axis=2)], axis=0)
    key_tiles = tile_store[:, 0].reshape(reach_span * blocks_here, BLOCK, width)
    value_tiles = tile_store[:, 1].reshape(reach_span * blocks_here, BLOCK, width)
    chosen = lax.dynamic_index_in_dim(selected, group_index, 1, keepdims=False)
    live_mask = lax.dynamic_index_in_dim(live_slots, group_index, 1, keepdims=False)
    block_ids = ctx_index * blocks_here + jnp.arange(blocks_here, dtype=jnp.int32)
    local_block = chosen % blocks_here
    per_part = blocks_here // parts_count
    rolled_block = (local_block // per_part - part_index) % parts_count * per_part + local_block % per_part
    slot_index = (ctx_index - chosen // blocks_here) * blocks_here + rolled_block
    pair_count = blocks_here // 2

    def accumulate(running, inputs):
        q_pair, do_pair, slot_pair, chosen_pair, live_pair, block_pair = inputs
        k_sel = key_tiles[slot_pair].reshape(2, -1, width)
        v_sel = value_tiles[slot_pair].reshape(2, -1, width)
        allowed = jax.vmap(visible_mask, in_axes=(0, 0, 0, None))(
            chosen_pair, live_pair, block_pair, BLOCK
        )
        query_part, key_part, value_part = tile_grads(
            q_pair, do_pair, k_sel, v_sel, allowed, inv_root
        )
        stacked = jnp.stack([key_part, value_part]).reshape(2, -1, BLOCK, width)
        running = running.at[:, slot_pair.reshape(-1)].add(stacked)
        return (running, query_part)

    initial = jnp.zeros((2, reach_span * blocks_here, BLOCK, width), jnp.float32)
    inputs = (
        queries.reshape(pair_count, 2, BLOCK, heads_here, width),
        out_grad.reshape(pair_count, 2, BLOCK, heads_here, width),
        slot_index.reshape(pair_count, 2, -1),
        chosen.reshape(pair_count, 2, -1),
        live_mask.reshape(pair_count, 2, -1),
        block_ids.reshape(pair_count, 2),
    )
    grads, query_parts = lax.scan(accumulate, initial, inputs)
    grads = grads.reshape(2, reach_span, tokens_here, width)
    sent = grads.astype(jnp.bfloat16)
    parts = grads[:, :, :quarter]
    for step in range(1, parts_count):
        piece = sent[:, :, step * quarter:(step + 1) * quarter]
        parts = parts + cycled(piece, "sub", step).astype(jnp.float32)
    running = parts[:, 0]
    for offset in range(1, reach_span):
        running = running + shifted_2(
            parts[:, offset].astype(jnp.bfloat16), "ctx", -offset
        ).astype(jnp.float32)
    mine = running.astype(jnp.bfloat16)
    by_part = jnp.stack([mine] + [cycled(mine, "sub", -step) for step in range(1, parts_count)])
    by_group = jnp.stack([by_part] + [cycled(by_part, "grp", -step) for step in range(1, groups)])
    part_order = (jnp.arange(parts_count) - part_index) % parts_count
    group_order = (jnp.arange(groups) - group_index) % groups
    ordered = jnp.take(jnp.take(by_group, group_order, axis=0), part_order, axis=1)
    summed = jnp.transpose(ordered, (2, 0, 1, 3, 4)).reshape(2, groups, tokens_here, width)
    summed = summed.astype(jnp.float32)
    query_grad = query_parts.reshape(tokens_here, heads_here, width)
    return (query_grad, summed[0], summed[1])


def solution(mesh):
    ctx_count, head_count = mesh.devices.shape
    groups = 4
    split = Mesh(
        np.asarray(mesh.devices).reshape(ctx_count, groups, head_count // groups),
        ("ctx", "grp", "sub"),
    )
    heads = ("grp", "sub")
    return jax.shard_map(
        per_device,
        mesh=split,
        in_specs=(
            P("ctx", heads, None),
            P(None, "ctx", None),
            P(None, "ctx", None),
            P("ctx", heads, None),
            P("ctx", None, None),
            P("ctx", None, None),
        ),
        out_specs=(P("ctx", heads, None), P(None, "ctx", None), P(None, "ctx", None)),
        check_vma=False,
    )
```

```python
import functools

import jax
import jax.numpy as jnp
import numpy as np
from jax import lax
from jax.experimental import pallas as pl
from jax.experimental.pallas import tpu as pltpu
from jax.sharding import Mesh
from jax.sharding import PartitionSpec as P

HPG = 16
BLOCK = 64
REACH = 6


def shifted_2(value, axis, steps):
    count = lax.axis_size(axis)
    leading, last = (max(0, -steps), min(count, count - steps))
    return lax.ppermute(value, axis, [(source, source + steps) for source in range(leading, last)])


def cycled(value, axis, steps):
    count = lax.axis_size(axis)
    return lax.ppermute(value, axis, [(source, (source + steps) % count) for source in range(count)])


def block_kernel(slots_ref, q_ref, do_ref, code_ref, k_ref, v_ref, dq_ref, dk_ref, dv_ref,
                 k_sel, v_sel, *, inv_root, heads_here):
    step = pl.program_id(0)
    slots = k_sel.shape[0] // BLOCK

    @pl.when(step == 0)
    def _():
        dk_ref[...] = jnp.zeros_like(dk_ref)
        dv_ref[...] = jnp.zeros_like(dv_ref)

    for slot in range(slots):
        start = pl.multiple_of(slots_ref[step, slot] * BLOCK, BLOCK)
        k_sel[slot * BLOCK:(slot + 1) * BLOCK, :] = k_ref[pl.ds(start, BLOCK), :]
        v_sel[slot * BLOCK:(slot + 1) * BLOCK, :] = v_ref[pl.ds(start, BLOCK), :]
    q = q_ref[...]
    do = do_ref[...]
    keys = k_sel[...]
    values = v_sel[...]
    rows, cols = q.shape[0], keys.shape[0]
    scores = lax.dot_general(
        q, keys, (((1,), (1,)), ((), ())), preferred_element_type=jnp.float32
    ) * inv_root
    code = code_ref[...]
    query_pos = lax.broadcasted_iota(jnp.int32, (rows, cols), 0) // heads_here
    key_pos = lax.broadcasted_iota(jnp.int32, (rows, cols), 1) % BLOCK
    allowed = (code == 2) | ((code == 1) & (query_pos >= key_pos))
    scores = jnp.where(allowed, scores, -1e30)
    row_max = jnp.max(scores, axis=1, keepdims=True)
    shifted = jnp.exp(scores - row_max)
    weights = shifted / jnp.sum(shifted, axis=1, keepdims=True)
    weights_b = weights.astype(jnp.bfloat16)
    output = jnp.dot(weights_b, values, preferred_element_type=jnp.float32)
    row_delta = jnp.sum(do.astype(jnp.float32) * output, axis=1, keepdims=True)
    prob_grad = lax.dot_general(
        do, values, (((1,), (1,)), ((), ())), preferred_element_type=jnp.float32
    )
    score_b = (weights * (prob_grad - row_delta)).astype(jnp.bfloat16)
    query_part = jnp.dot(score_b, keys, preferred_element_type=jnp.float32) * inv_root
    dq_ref[...] = query_part.astype(jnp.bfloat16)
    key_part = lax.dot_general(
        score_b, q, (((0,), (0,)), ((), ())), preferred_element_type=jnp.float32
    ) * inv_root
    value_part = lax.dot_general(
        weights_b, do, (((0,), (0,)), ((), ())), preferred_element_type=jnp.float32
    )
    for slot in range(slots):
        start = pl.multiple_of(slots_ref[step, slot] * BLOCK, BLOCK)
        dk_ref[pl.ds(start, BLOCK), :] += key_part[slot * BLOCK:(slot + 1) * BLOCK]
        dv_ref[pl.ds(start, BLOCK), :] += value_part[slot * BLOCK:(slot + 1) * BLOCK]


def local_grads(queries, out_grad, key_tiles, value_tiles, slot_index, code, inv_root,
                interpret=False):
    tokens_here, heads_here, width = queries.shape
    blocks_here, slots = slot_index.shape
    rows = BLOCK * heads_here
    store = key_tiles.shape[0] * BLOCK
    cols = slots * BLOCK
    code_cols = jnp.repeat(code.astype(jnp.int32), BLOCK, axis=1).reshape(blocks_here, 1, cols)
    kernel = functools.partial(block_kernel, inv_root=inv_root, heads_here=heads_here)
    whole = lambda step, slots_ref: (0, 0)
    per_block = lambda step, slots_ref: (step, 0)
    query_grad, key_grad, value_grad = pl.pallas_call(
        kernel,
        grid_spec=pltpu.PrefetchScalarGridSpec(
            num_scalar_prefetch=1,
            grid=(blocks_here,),
            in_specs=[
                pl.BlockSpec((rows, width), per_block),
                pl.BlockSpec((rows, width), per_block),
                pl.BlockSpec((None, 1, cols), lambda step, slots_ref: (step, 0, 0)),
                pl.BlockSpec((store, width), whole),
                pl.BlockSpec((store, width), whole),
            ],
            out_specs=[
                pl.BlockSpec((rows, width), per_block),
                pl.BlockSpec((store, width), whole),
                pl.BlockSpec((store, width), whole),
            ],
            scratch_shapes=[
                pltpu.VMEM((cols, width), jnp.bfloat16),
                pltpu.VMEM((cols, width), jnp.bfloat16),
            ],
        ),
        out_shape=[
            jax.ShapeDtypeStruct((tokens_here * heads_here, width), jnp.bfloat16),
            jax.ShapeDtypeStruct((store, width), jnp.float32),
            jax.ShapeDtypeStruct((store, width), jnp.float32),
        ],
        compiler_params=pltpu.CompilerParams(dimension_semantics=("arbitrary",)),
        interpret=interpret,
    )(
        slot_index.astype(jnp.int32),
        queries.reshape(tokens_here * heads_here, width),
        out_grad.reshape(tokens_here * heads_here, width),
        code_cols,
        key_tiles.reshape(store, width),
        value_tiles.reshape(store, width),
    )
    return query_grad.reshape(tokens_here, heads_here, width), key_grad, value_grad


def per_device(queries, key_rows, value_rows, out_grad, selected, live_slots):
    tokens_here, heads_here, width = queries.shape
    groups = key_rows.shape[0]
    blocks_here = tokens_here // BLOCK
    reach_span = REACH + 1
    inv_root = width ** (-0.5)
    ctx_index = lax.axis_index("ctx")
    group_index = lax.axis_index("grp")
    part_index = lax.axis_index("sub")
    parts_count = lax.axis_size("sub")
    quarter = tokens_here // parts_count
    own_tiles = jnp.stack(
        [
            lax.dynamic_index_in_dim(key_rows, group_index, 0, keepdims=False),
            lax.dynamic_index_in_dim(value_rows, group_index, 0, keepdims=False),
        ]
    )
    rolled = jnp.roll(own_tiles, -part_index * quarter, axis=1)
    own_part = rolled[:, :quarter]
    fetched = jnp.stack([shifted_2(own_part, "ctx", offset) for offset in range(1, reach_span)])
    pieces = [fetched] + [cycled(fetched, "sub", -step) for step in range(1, parts_count)]
    tile_store = jnp.concatenate([rolled[None], jnp.concatenate(pieces, axis=2)], axis=0)
    key_tiles = tile_store[:, 0].reshape(reach_span * blocks_here, BLOCK, width)
    value_tiles = tile_store[:, 1].reshape(reach_span * blocks_here, BLOCK, width)
    chosen = lax.dynamic_index_in_dim(selected, group_index, 1, keepdims=False)
    live_mask = lax.dynamic_index_in_dim(live_slots, group_index, 1, keepdims=False)
    block_ids = ctx_index * blocks_here + jnp.arange(blocks_here, dtype=jnp.int32)
    local_block = chosen % blocks_here
    per_part = blocks_here // parts_count
    rolled_block = (local_block // per_part - part_index) % parts_count * per_part + local_block % per_part
    slot_index = (ctx_index - chosen // blocks_here) * blocks_here + rolled_block
    slot_index = jnp.clip(slot_index, 0, reach_span * blocks_here - 1)
    code = jnp.where(live_mask == 1, jnp.where(chosen < block_ids[:, None], 2, 1), 0)
    query_grad, key_grad, value_grad = local_grads(
        queries, out_grad, key_tiles, value_tiles, slot_index, code, inv_root
    )
    grads = jnp.stack([key_grad, value_grad]).reshape(2, reach_span, tokens_here, width)
    sent = grads.astype(jnp.bfloat16)
    parts = grads[:, :, :quarter]
    for step in range(1, parts_count):
        piece = sent[:, :, step * quarter:(step + 1) * quarter]
        parts = parts + cycled(piece, "sub", step).astype(jnp.float32)
    running = parts[:, 0]
    for offset in range(1, reach_span):
        running = running + shifted_2(
            parts[:, offset].astype(jnp.bfloat16), "ctx", -offset
        ).astype(jnp.float32)
    mine = running.astype(jnp.bfloat16)
    by_part = jnp.stack([mine] + [cycled(mine, "sub", -step) for step in range(1, parts_count)])
    by_group = jnp.stack([by_part] + [cycled(by_part, "grp", -step) for step in range(1, groups)])
    part_order = (jnp.arange(parts_count) - part_index) % parts_count
    group_order = (jnp.arange(groups) - group_index) % groups
    ordered = jnp.take(jnp.take(by_group, group_order, axis=0), part_order, axis=1)
    summed = jnp.transpose(ordered, (2, 0, 1, 3, 4)).reshape(2, groups, tokens_here, width)
    summed = summed.astype(jnp.float32)
    return (query_grad, summed[0], summed[1])


def solution(mesh):
    ctx_count, head_count = mesh.devices.shape
    groups = 4
    split = Mesh(
        np.asarray(mesh.devices).reshape(ctx_count, groups, head_count // groups),
        ("ctx", "grp", "sub"),
    )
    heads = ("grp", "sub")
    return jax.shard_map(
        per_device,
        mesh=split,
        in_specs=(
            P("ctx", heads, None),
            P(None, "ctx", None),
            P(None, "ctx", None),
            P("ctx", heads, None),
            P("ctx", None, None),
            P("ctx", None, None),
        ),
        out_specs=(P("ctx", heads, None), P(None, "ctx", None), P(None, "ctx", None)),
        check_vma=False,
    )
```

```python
import functools

import jax
import jax.numpy as jnp
import numpy as np
from jax import lax
from jax.experimental import pallas as pl
from jax.experimental.pallas import tpu as pltpu
from jax.sharding import Mesh
from jax.sharding import PartitionSpec as P

HPG = 16
BLOCK = 64
REACH = 6


def shifted_2(value, axis, steps):
    count = lax.axis_size(axis)
    leading, last = (max(0, -steps), min(count, count - steps))
    return lax.ppermute(value, axis, [(source, source + steps) for source in range(leading, last)])


def cycled(value, axis, steps):
    count = lax.axis_size(axis)
    return lax.ppermute(value, axis, [(source, (source + steps) % count) for source in range(count)])


def block_kernel(slots_ref, q_ref, do_ref, code_ref, k_ref, v_ref, dq_ref, dk_ref, dv_ref,
                 k_sel, v_sel, *, inv_root, heads_here):
    step = pl.program_id(0)
    slots = k_sel.shape[0] // BLOCK

    @pl.when(step == 0)
    def _():
        dk_ref[...] = jnp.zeros_like(dk_ref)
        dv_ref[...] = jnp.zeros_like(dv_ref)

    for slot in range(slots):
        start = pl.multiple_of(slots_ref[step, slot] * BLOCK, BLOCK)
        k_sel[slot * BLOCK:(slot + 1) * BLOCK, :] = k_ref[pl.ds(start, BLOCK), :]
        v_sel[slot * BLOCK:(slot + 1) * BLOCK, :] = v_ref[pl.ds(start, BLOCK), :]
    q = q_ref[...]
    do = do_ref[...]
    keys = k_sel[...]
    values = v_sel[...]
    rows, cols = q.shape[0], keys.shape[0]
    scores = lax.dot_general(
        q, keys, (((1,), (1,)), ((), ())), preferred_element_type=jnp.float32
    ) * inv_root
    code = code_ref[...]
    query_pos = lax.broadcasted_iota(jnp.int32, (rows, cols), 0) // heads_here
    key_pos = lax.broadcasted_iota(jnp.int32, (rows, cols), 1) % BLOCK
    allowed = (code == 2) | ((code == 1) & (query_pos >= key_pos))
    scores = jnp.where(allowed, scores, -1e30)
    row_max = jnp.max(scores, axis=1, keepdims=True)
    shifted = jnp.exp(scores - row_max)
    weights = shifted * (1.0 / jnp.sum(shifted, axis=1, keepdims=True))
    weights_b = weights.astype(jnp.bfloat16)
    output = jnp.dot(weights_b, values, preferred_element_type=jnp.float32)
    row_delta = jnp.sum(do.astype(jnp.float32) * output, axis=1, keepdims=True)
    prob_grad = lax.dot_general(
        do, values, (((1,), (1,)), ((), ())), preferred_element_type=jnp.float32
    )
    score_b = (weights * (prob_grad - row_delta)).astype(jnp.bfloat16)
    query_part = jnp.dot(score_b, keys, preferred_element_type=jnp.float32) * inv_root
    dq_ref[...] = query_part.astype(jnp.bfloat16)
    key_part = lax.dot_general(
        score_b, q, (((0,), (0,)), ((), ())), preferred_element_type=jnp.float32
    ) * inv_root
    value_part = lax.dot_general(
        weights_b, do, (((0,), (0,)), ((), ())), preferred_element_type=jnp.float32
    )
    for slot in range(slots):
        start = pl.multiple_of(slots_ref[step, slot] * BLOCK, BLOCK)
        dk_ref[pl.ds(start, BLOCK), :] += key_part[slot * BLOCK:(slot + 1) * BLOCK]
        dv_ref[pl.ds(start, BLOCK), :] += value_part[slot * BLOCK:(slot + 1) * BLOCK]


def local_grads(queries, out_grad, key_tiles, value_tiles, slot_index, code, inv_root,
                interpret=False):
    tokens_here, heads_here, width = queries.shape
    blocks_here, slots = slot_index.shape
    rows = BLOCK * heads_here
    store = key_tiles.shape[0] * BLOCK
    cols = slots * BLOCK
    code_cols = jnp.repeat(code.astype(jnp.int32), BLOCK, axis=1).reshape(blocks_here, 1, cols)
    kernel = functools.partial(block_kernel, inv_root=inv_root, heads_here=heads_here)
    whole = lambda step, slots_ref: (0, 0)
    per_block = lambda step, slots_ref: (step, 0)
    query_grad, key_grad, value_grad = pl.pallas_call(
        kernel,
        grid_spec=pltpu.PrefetchScalarGridSpec(
            num_scalar_prefetch=1,
            grid=(blocks_here,),
            in_specs=[
                pl.BlockSpec((rows, width), per_block),
                pl.BlockSpec((rows, width), per_block),
                pl.BlockSpec((None, 1, cols), lambda step, slots_ref: (step, 0, 0)),
                pl.BlockSpec((store, width), whole),
                pl.BlockSpec((store, width), whole),
            ],
            out_specs=[
                pl.BlockSpec((rows, width), per_block),
                pl.BlockSpec((store, width), whole),
                pl.BlockSpec((store, width), whole),
            ],
            scratch_shapes=[
                pltpu.VMEM((cols, width), jnp.bfloat16),
                pltpu.VMEM((cols, width), jnp.bfloat16),
            ],
        ),
        out_shape=[
            jax.ShapeDtypeStruct((tokens_here * heads_here, width), jnp.bfloat16),
            jax.ShapeDtypeStruct((store, width), jnp.float32),
            jax.ShapeDtypeStruct((store, width), jnp.float32),
        ],
        compiler_params=pltpu.CompilerParams(dimension_semantics=("arbitrary",)),
        interpret=interpret,
    )(
        slot_index.astype(jnp.int32),
        queries.reshape(tokens_here * heads_here, width),
        out_grad.reshape(tokens_here * heads_here, width),
        code_cols,
        key_tiles.reshape(store, width),
        value_tiles.reshape(store, width),
    )
    return query_grad.reshape(tokens_here, heads_here, width), key_grad, value_grad


def per_device(queries, key_rows, value_rows, out_grad, selected, live_slots):
    tokens_here, heads_here, width = queries.shape
    groups = key_rows.shape[0]
    blocks_here = tokens_here // BLOCK
    reach_span = REACH + 1
    inv_root = width ** (-0.5)
    ctx_index = lax.axis_index("ctx")
    group_index = lax.axis_index("grp")
    part_index = lax.axis_index("sub")
    parts_count = lax.axis_size("sub")
    quarter = tokens_here // parts_count
    own_tiles = jnp.stack(
        [
            lax.dynamic_index_in_dim(key_rows, group_index, 0, keepdims=False),
            lax.dynamic_index_in_dim(value_rows, group_index, 0, keepdims=False),
        ]
    )
    rolled = jnp.roll(own_tiles, -part_index * quarter, axis=1)
    own_part = rolled[:, :quarter]
    fetched = jnp.stack([shifted_2(own_part, "ctx", offset) for offset in range(1, reach_span)])
    pieces = [fetched] + [cycled(fetched, "sub", -step) for step in range(1, parts_count)]
    tile_store = jnp.concatenate([rolled[None], jnp.concatenate(pieces, axis=2)], axis=0)
    key_tiles = tile_store[:, 0].reshape(reach_span * blocks_here, BLOCK, width)
    value_tiles = tile_store[:, 1].reshape(reach_span * blocks_here, BLOCK, width)
    chosen = lax.dynamic_index_in_dim(selected, group_index, 1, keepdims=False)
    live_mask = lax.dynamic_index_in_dim(live_slots, group_index, 1, keepdims=False)
    block_ids = ctx_index * blocks_here + jnp.arange(blocks_here, dtype=jnp.int32)
    local_block = chosen % blocks_here
    per_part = blocks_here // parts_count
    rolled_block = (local_block // per_part - part_index) % parts_count * per_part + local_block % per_part
    slot_index = (ctx_index - chosen // blocks_here) * blocks_here + rolled_block
    slot_index = jnp.clip(slot_index, 0, reach_span * blocks_here - 1)
    code = jnp.where(live_mask == 1, jnp.where(chosen < block_ids[:, None], 2, 1), 0)
    query_grad, key_grad, value_grad = local_grads(
        queries, out_grad, key_tiles, value_tiles, slot_index, code, inv_root
    )
    grads = jnp.stack([key_grad, value_grad]).reshape(2, reach_span, tokens_here, width)
    sent = grads.astype(jnp.bfloat16)
    parts = grads[:, :, :quarter]
    for step in range(1, parts_count):
        piece = sent[:, :, step * quarter:(step + 1) * quarter]
        parts = parts + cycled(piece, "sub", step).astype(jnp.float32)
    running = parts[:, 0]
    for offset in range(1, reach_span):
        running = running + shifted_2(
            parts[:, offset].astype(jnp.bfloat16), "ctx", -offset
        ).astype(jnp.float32)
    mine = running.astype(jnp.bfloat16)
    by_group = jnp.stack([mine] + [cycled(mine, "grp", -step) for step in range(1, groups)])
    by_part = jnp.stack([by_group] + [cycled(by_group, "sub", -step) for step in range(1, parts_count)])
    part_order = (jnp.arange(parts_count) - part_index) % parts_count
    group_order = (jnp.arange(groups) - group_index) % groups
    ordered = jnp.take(jnp.take(by_part, part_order, axis=0), group_order, axis=1)
    ordered = jnp.transpose(ordered, (1, 0, 2, 3, 4))
    summed = jnp.transpose(ordered, (2, 0, 1, 3, 4)).reshape(2, groups, tokens_here, width)
    summed = summed.astype(jnp.float32)
    return (query_grad, summed[0], summed[1])


def solution(mesh):
    ctx_count, head_count = mesh.devices.shape
    groups = 4
    split = Mesh(
        np.asarray(mesh.devices).reshape(ctx_count, groups, head_count // groups),
        ("ctx", "grp", "sub"),
    )
    heads = ("grp", "sub")
    return jax.shard_map(
        per_device,
        mesh=split,
        in_specs=(
            P("ctx", heads, None),
            P(None, "ctx", None),
            P(None, "ctx", None),
            P("ctx", heads, None),
            P("ctx", None, None),
            P("ctx", None, None),
        ),
        out_specs=(P("ctx", heads, None), P(None, "ctx", None), P(None, "ctx", None)),
        check_vma=False,
    )
```

```python
import functools

import jax
import jax.numpy as jnp
import numpy as np
from jax import lax
from jax.experimental import pallas as pl
from jax.experimental.pallas import tpu as pltpu
from jax.sharding import Mesh
from jax.sharding import PartitionSpec as P

HPG = 16
BLOCK = 64
REACH = 6


def shifted_2(value, axis, steps):
    count = lax.axis_size(axis)
    leading, last = (max(0, -steps), min(count, count - steps))
    return lax.ppermute(value, axis, [(source, source + steps) for source in range(leading, last)])


def cycled(value, axis, steps):
    count = lax.axis_size(axis)
    return lax.ppermute(value, axis, [(source, (source + steps) % count) for source in range(count)])


def block_kernel(slots_ref, q_ref, do_ref, code_ref, k_ref, v_ref, dq_ref, dk_ref, dv_ref,
                 k_sel, v_sel, *, inv_root, heads_here):
    step = pl.program_id(0)
    slots = k_sel.shape[0] // BLOCK

    @pl.when(step == 0)
    def _():
        dk_ref[...] = jnp.zeros_like(dk_ref)
        dv_ref[...] = jnp.zeros_like(dv_ref)

    for slot in range(slots):
        start = pl.multiple_of(slots_ref[step, slot] * BLOCK, BLOCK)
        k_sel[slot * BLOCK:(slot + 1) * BLOCK, :] = k_ref[pl.ds(start, BLOCK), :]
        v_sel[slot * BLOCK:(slot + 1) * BLOCK, :] = v_ref[pl.ds(start, BLOCK), :]
    q = q_ref[...]
    do = do_ref[...]
    keys = k_sel[...]
    values = v_sel[...]
    rows, cols = q.shape[0], keys.shape[0]
    scores = lax.dot_general(
        q, keys, (((1,), (1,)), ((), ())), preferred_element_type=jnp.float32
    ) * inv_root
    code = code_ref[...]
    query_pos = lax.broadcasted_iota(jnp.int32, (rows, cols), 0) // heads_here
    key_pos = lax.broadcasted_iota(jnp.int32, (rows, cols), 1) % BLOCK
    allowed = (code == 2) | ((code == 1) & (query_pos >= key_pos))
    scores = jnp.where(allowed, scores, -1e30)
    row_max = jnp.max(scores, axis=1, keepdims=True)
    shifted = jnp.exp(scores - row_max)
    weights = shifted * (1.0 / jnp.sum(shifted, axis=1, keepdims=True))
    weights_b = weights.astype(jnp.bfloat16)
    output = jnp.dot(weights_b, values, preferred_element_type=jnp.float32)
    row_delta = jnp.sum(do.astype(jnp.float32) * output, axis=1, keepdims=True)
    prob_grad = lax.dot_general(
        do, values, (((1,), (1,)), ((), ())), preferred_element_type=jnp.float32
    )
    score_b = (weights * (prob_grad - row_delta)).astype(jnp.bfloat16)
    query_part = jnp.dot(score_b, keys, preferred_element_type=jnp.float32) * inv_root
    dq_ref[...] = query_part.astype(jnp.bfloat16)
    key_part = lax.dot_general(
        score_b, q, (((0,), (0,)), ((), ())), preferred_element_type=jnp.float32
    ) * inv_root
    value_part = lax.dot_general(
        weights_b, do, (((0,), (0,)), ((), ())), preferred_element_type=jnp.float32
    )
    for slot in range(slots):
        start = pl.multiple_of(slots_ref[step, slot] * BLOCK, BLOCK)
        dk_ref[pl.ds(start, BLOCK), :] += key_part[slot * BLOCK:(slot + 1) * BLOCK]
        dv_ref[pl.ds(start, BLOCK), :] += value_part[slot * BLOCK:(slot + 1) * BLOCK]


def local_grads(queries, out_grad, key_tiles, value_tiles, slot_index, code, inv_root,
                interpret=False):
    tokens_here, heads_here, width = queries.shape
    blocks_here, slots = slot_index.shape
    rows = BLOCK * heads_here
    store = key_tiles.shape[0] * BLOCK
    cols = slots * BLOCK
    code_cols = jnp.repeat(code.astype(jnp.int32), BLOCK, axis=1).reshape(blocks_here, 1, cols)
    kernel = functools.partial(block_kernel, inv_root=inv_root, heads_here=heads_here)
    whole = lambda step, slots_ref: (0, 0)
    per_block = lambda step, slots_ref: (step, 0)
    query_grad, key_grad, value_grad = pl.pallas_call(
        kernel,
        grid_spec=pltpu.PrefetchScalarGridSpec(
            num_scalar_prefetch=1,
            grid=(blocks_here,),
            in_specs=[
                pl.BlockSpec((rows, width), per_block),
                pl.BlockSpec((rows, width), per_block),
                pl.BlockSpec((None, 1, cols), lambda step, slots_ref: (step, 0, 0)),
                pl.BlockSpec((store, width), whole),
                pl.BlockSpec((store, width), whole),
            ],
            out_specs=[
                pl.BlockSpec((rows, width), per_block),
                pl.BlockSpec((store, width), whole),
                pl.BlockSpec((store, width), whole),
            ],
            scratch_shapes=[
                pltpu.VMEM((cols, width), jnp.bfloat16),
                pltpu.VMEM((cols, width), jnp.bfloat16),
            ],
        ),
        out_shape=[
            jax.ShapeDtypeStruct((tokens_here * heads_here, width), jnp.bfloat16),
            jax.ShapeDtypeStruct((store, width), jnp.float32),
            jax.ShapeDtypeStruct((store, width), jnp.float32),
        ],
        compiler_params=pltpu.CompilerParams(dimension_semantics=("arbitrary",)),
        interpret=interpret,
    )(
        slot_index.astype(jnp.int32),
        queries.reshape(tokens_here * heads_here, width),
        out_grad.reshape(tokens_here * heads_here, width),
        code_cols,
        key_tiles.reshape(store, width),
        value_tiles.reshape(store, width),
    )
    return query_grad.reshape(tokens_here, heads_here, width), key_grad, value_grad


def per_device(queries, key_rows, value_rows, out_grad, selected, live_slots):
    tokens_here, heads_here, width = queries.shape
    groups = key_rows.shape[0]
    blocks_here = tokens_here // BLOCK
    reach_span = REACH + 1
    inv_root = width ** (-0.5)
    ctx_index = lax.axis_index("ctx")
    group_index = lax.axis_index("grp")
    part_index = lax.axis_index("sub")
    parts_count = lax.axis_size("sub")
    quarter = tokens_here // parts_count
    own_tiles = jnp.stack(
        [
            lax.dynamic_index_in_dim(key_rows, group_index, 0, keepdims=False),
            lax.dynamic_index_in_dim(value_rows, group_index, 0, keepdims=False),
        ]
    )
    rolled = jnp.roll(own_tiles, -part_index * quarter, axis=1)
    own_part = rolled[:, :quarter]
    fetched = jnp.stack([shifted_2(own_part, "ctx", offset) for offset in range(1, reach_span)])
    pieces = [fetched] + [cycled(fetched, "sub", -step) for step in range(1, parts_count)]
    tile_store = jnp.concatenate([rolled[None], jnp.concatenate(pieces, axis=2)], axis=0)
    key_tiles = tile_store[:, 0].reshape(reach_span * blocks_here, BLOCK, width)
    value_tiles = tile_store[:, 1].reshape(reach_span * blocks_here, BLOCK, width)
    chosen = lax.dynamic_index_in_dim(selected, group_index, 1, keepdims=False)
    live_mask = lax.dynamic_index_in_dim(live_slots, group_index, 1, keepdims=False)
    block_ids = ctx_index * blocks_here + jnp.arange(blocks_here, dtype=jnp.int32)
    local_block = chosen % blocks_here
    per_part = blocks_here // parts_count
    rolled_block = (local_block // per_part - part_index) % parts_count * per_part + local_block % per_part
    slot_index = (ctx_index - chosen // blocks_here) * blocks_here + rolled_block
    slot_index = jnp.clip(slot_index, 0, reach_span * blocks_here - 1)
    code = jnp.where(live_mask == 1, jnp.where(chosen < block_ids[:, None], 2, 1), 0)
    query_grad, key_grad, value_grad = local_grads(
        queries, out_grad, key_tiles, value_tiles, slot_index, code, inv_root
    )
    grads = jnp.stack([key_grad, value_grad]).reshape(2, reach_span, tokens_here, width)
    sent = grads.astype(jnp.bfloat16)
    split = REACH // 2 + 1
    running = None
    for lo, hi in ((split, reach_span), (0, split)):
        part = grads[:, lo:hi, :quarter]
        for step in range(1, parts_count):
            piece = sent[:, lo:hi, step * quarter:(step + 1) * quarter]
            part = part + cycled(piece, "sub", step).astype(jnp.float32)
        for offset in range(lo, hi):
            term = part[:, offset - lo]
            if offset:
                term = shifted_2(term.astype(jnp.bfloat16), "ctx", -offset).astype(jnp.float32)
            running = term if running is None else running + term
    mine = running.astype(jnp.bfloat16)
    by_group = jnp.stack([mine] + [cycled(mine, "grp", -step) for step in range(1, groups)])
    by_part = jnp.stack([by_group] + [cycled(by_group, "sub", -step) for step in range(1, parts_count)])
    part_order = (jnp.arange(parts_count) - part_index) % parts_count
    group_order = (jnp.arange(groups) - group_index) % groups
    ordered = jnp.take(jnp.take(by_part, part_order, axis=0), group_order, axis=1)
    ordered = jnp.transpose(ordered, (1, 0, 2, 3, 4))
    summed = jnp.transpose(ordered, (2, 0, 1, 3, 4)).reshape(2, groups, tokens_here, width)
    summed = summed.astype(jnp.float32)
    return (query_grad, summed[0], summed[1])


def solution(mesh):
    ctx_count, head_count = mesh.devices.shape
    groups = 4
    split = Mesh(
        np.asarray(mesh.devices).reshape(ctx_count, groups, head_count // groups),
        ("ctx", "grp", "sub"),
    )
    heads = ("grp", "sub")
    return jax.shard_map(
        per_device,
        mesh=split,
        in_specs=(
            P("ctx", heads, None),
            P(None, "ctx", None),
            P(None, "ctx", None),
            P("ctx", heads, None),
            P("ctx", None, None),
            P("ctx", None, None),
        ),
        out_specs=(P("ctx", heads, None), P(None, "ctx", None), P(None, "ctx", None)),
        check_vma=False,
    )
```

```python
import functools

import jax
import jax.numpy as jnp
import numpy as np
from jax import lax
from jax.experimental import pallas as pl
from jax.experimental.pallas import tpu as pltpu
from jax.sharding import Mesh
from jax.sharding import PartitionSpec as P

HPG = 16
BLOCK = 64
REACH = 6


def shifted_2(value, axis, steps):
    count = lax.axis_size(axis)
    leading, last = (max(0, -steps), min(count, count - steps))
    return lax.ppermute(value, axis, [(source, source + steps) for source in range(leading, last)])


def cycled(value, axis, steps):
    count = lax.axis_size(axis)
    return lax.ppermute(value, axis, [(source, (source + steps) % count) for source in range(count)])


def block_kernel(slots_ref, q_ref, do_ref, code_ref, k_ref, v_ref, dq_ref, dk_ref, dv_ref,
                 k_sel, v_sel, *, inv_root, heads_here):
    step = pl.program_id(0)
    slots = k_sel.shape[0] // BLOCK

    @pl.when(step == 0)
    def _():
        dk_ref[...] = jnp.zeros_like(dk_ref)
        dv_ref[...] = jnp.zeros_like(dv_ref)

    for slot in range(slots):
        start = pl.multiple_of(slots_ref[step, slot] * BLOCK, BLOCK)
        k_sel[slot * BLOCK:(slot + 1) * BLOCK, :] = k_ref[pl.ds(start, BLOCK), :]
        v_sel[slot * BLOCK:(slot + 1) * BLOCK, :] = v_ref[pl.ds(start, BLOCK), :]
    q = q_ref[...]
    do = do_ref[...]
    keys = k_sel[...]
    values = v_sel[...]
    rows, cols = q.shape[0], keys.shape[0]
    scores = lax.dot_general(
        q, keys, (((1,), (1,)), ((), ())), preferred_element_type=jnp.float32
    ) * inv_root
    query_pos = lax.broadcasted_iota(jnp.int32, (rows, 1), 0) // heads_here
    allowed = query_pos >= code_ref[...]
    scores = jnp.where(allowed, scores, -1e30)
    row_max = jnp.max(scores, axis=1, keepdims=True)
    shifted = jnp.exp(scores - row_max)
    weights = shifted * (1.0 / jnp.sum(shifted, axis=1, keepdims=True))
    weights_b = weights.astype(jnp.bfloat16)
    output = jnp.dot(weights_b, values, preferred_element_type=jnp.float32)
    row_delta = jnp.sum(do.astype(jnp.float32) * output, axis=1, keepdims=True)
    prob_grad = lax.dot_general(
        do, values, (((1,), (1,)), ((), ())), preferred_element_type=jnp.float32
    )
    score_b = (weights * (prob_grad - row_delta)).astype(jnp.bfloat16)
    query_part = jnp.dot(score_b, keys, preferred_element_type=jnp.float32) * inv_root
    dq_ref[...] = query_part.astype(jnp.bfloat16)
    key_part = lax.dot_general(
        score_b, q, (((0,), (0,)), ((), ())), preferred_element_type=jnp.float32
    ) * inv_root
    value_part = lax.dot_general(
        weights_b, do, (((0,), (0,)), ((), ())), preferred_element_type=jnp.float32
    )
    for slot in range(slots):
        start = pl.multiple_of(slots_ref[step, slot] * BLOCK, BLOCK)
        dk_ref[pl.ds(start, BLOCK), :] += key_part[slot * BLOCK:(slot + 1) * BLOCK]
        dv_ref[pl.ds(start, BLOCK), :] += value_part[slot * BLOCK:(slot + 1) * BLOCK]


def local_grads(queries, out_grad, key_tiles, value_tiles, slot_index, code, inv_root,
                interpret=False):
    tokens_here, heads_here, width = queries.shape
    blocks_here, slots = slot_index.shape
    rows = BLOCK * heads_here
    store = key_tiles.shape[0] * BLOCK
    cols = slots * BLOCK
    key_pos = jnp.tile(jnp.arange(BLOCK, dtype=jnp.int32), slots)[None, :]
    code_cols = jnp.repeat(code.astype(jnp.int32), BLOCK, axis=1)
    code_cols = jnp.where(code_cols == 2, 0, jnp.where(code_cols == 1, key_pos, BLOCK))
    code_cols = code_cols.reshape(blocks_here, 1, cols)
    kernel = functools.partial(block_kernel, inv_root=inv_root, heads_here=heads_here)
    whole = lambda step, slots_ref: (0, 0)
    per_block = lambda step, slots_ref: (step, 0)
    query_grad, key_grad, value_grad = pl.pallas_call(
        kernel,
        grid_spec=pltpu.PrefetchScalarGridSpec(
            num_scalar_prefetch=1,
            grid=(blocks_here,),
            in_specs=[
                pl.BlockSpec((rows, width), per_block),
                pl.BlockSpec((rows, width), per_block),
                pl.BlockSpec((None, 1, cols), lambda step, slots_ref: (step, 0, 0)),
                pl.BlockSpec((store, width), whole),
                pl.BlockSpec((store, width), whole),
            ],
            out_specs=[
                pl.BlockSpec((rows, width), per_block),
                pl.BlockSpec((store, width), whole),
                pl.BlockSpec((store, width), whole),
            ],
            scratch_shapes=[
                pltpu.VMEM((cols, width), jnp.bfloat16),
                pltpu.VMEM((cols, width), jnp.bfloat16),
            ],
        ),
        out_shape=[
            jax.ShapeDtypeStruct((tokens_here * heads_here, width), jnp.bfloat16),
            jax.ShapeDtypeStruct((store, width), jnp.float32),
            jax.ShapeDtypeStruct((store, width), jnp.float32),
        ],
        compiler_params=pltpu.CompilerParams(dimension_semantics=("arbitrary",)),
        interpret=interpret,
    )(
        slot_index.astype(jnp.int32),
        queries.reshape(tokens_here * heads_here, width),
        out_grad.reshape(tokens_here * heads_here, width),
        code_cols,
        key_tiles.reshape(store, width),
        value_tiles.reshape(store, width),
    )
    return query_grad.reshape(tokens_here, heads_here, width), key_grad, value_grad


def per_device(queries, key_rows, value_rows, out_grad, selected, live_slots):
    tokens_here, heads_here, width = queries.shape
    groups = key_rows.shape[0]
    blocks_here = tokens_here // BLOCK
    reach_span = REACH + 1
    inv_root = width ** (-0.5)
    ctx_index = lax.axis_index("ctx")
    group_index = lax.axis_index("grp")
    part_index = lax.axis_index("sub")
    parts_count = lax.axis_size("sub")
    quarter = tokens_here // parts_count
    own_tiles = jnp.stack(
        [
            lax.dynamic_index_in_dim(key_rows, group_index, 0, keepdims=False),
            lax.dynamic_index_in_dim(value_rows, group_index, 0, keepdims=False),
        ]
    )
    rolled = jnp.roll(own_tiles, -part_index * quarter, axis=1)
    own_part = rolled[:, :quarter]
    fetched = jnp.stack([shifted_2(own_part, "ctx", offset) for offset in range(1, reach_span)])
    pieces = [fetched] + [cycled(fetched, "sub", -step) for step in range(1, parts_count)]
    tile_store = jnp.concatenate([rolled[None], jnp.concatenate(pieces, axis=2)], axis=0)
    key_tiles = tile_store[:, 0].reshape(reach_span * blocks_here, BLOCK, width)
    value_tiles = tile_store[:, 1].reshape(reach_span * blocks_here, BLOCK, width)
    chosen = lax.dynamic_index_in_dim(selected, group_index, 1, keepdims=False)
    live_mask = lax.dynamic_index_in_dim(live_slots, group_index, 1, keepdims=False)
    block_ids = ctx_index * blocks_here + jnp.arange(blocks_here, dtype=jnp.int32)
    local_block = chosen % blocks_here
    per_part = blocks_here // parts_count
    rolled_block = (local_block // per_part - part_index) % parts_count * per_part + local_block % per_part
    slot_index = (ctx_index - chosen // blocks_here) * blocks_here + rolled_block
    slot_index = jnp.clip(slot_index, 0, reach_span * blocks_here - 1)
    code = jnp.where(live_mask == 1, jnp.where(chosen < block_ids[:, None], 2, 1), 0)
    query_grad, key_grad, value_grad = local_grads(
        queries, out_grad, key_tiles, value_tiles, slot_index, code, inv_root
    )
    grads = jnp.stack([key_grad, value_grad]).reshape(2, reach_span, tokens_here, width)
    sent = grads.astype(jnp.bfloat16)
    split = REACH // 2 + 1
    running = None
    for lo, hi in ((split, reach_span), (0, split)):
        part = grads[:, lo:hi, :quarter]
        for step in range(1, parts_count):
            piece = sent[:, lo:hi, step * quarter:(step + 1) * quarter]
            part = part + cycled(piece, "sub", step).astype(jnp.float32)
        for offset in range(lo, hi):
            term = part[:, offset - lo]
            if offset:
                term = shifted_2(term.astype(jnp.bfloat16), "ctx", -offset).astype(jnp.float32)
            running = term if running is None else running + term
    mine = running.astype(jnp.bfloat16)
    by_group = jnp.stack([mine] + [cycled(mine, "grp", -step) for step in range(1, groups)])
    by_part = jnp.stack([by_group] + [cycled(by_group, "sub", -step) for step in range(1, parts_count)])
    part_order = (jnp.arange(parts_count) - part_index) % parts_count
    group_order = (jnp.arange(groups) - group_index) % groups
    flat_order = (part_order[None, :] * groups + group_order[:, None]).reshape(-1)
    ordered = jnp.take(by_part.reshape((parts_count * groups,) + mine.shape), flat_order, axis=0)
    ordered = ordered.reshape((groups, parts_count) + mine.shape)
    summed = jnp.transpose(ordered, (2, 0, 1, 3, 4)).reshape(2, groups, tokens_here, width)
    summed = summed.astype(jnp.float32)
    return (query_grad, summed[0], summed[1])


def solution(mesh):
    ctx_count, head_count = mesh.devices.shape
    groups = 4
    split = Mesh(
        np.asarray(mesh.devices).reshape(ctx_count, groups, head_count // groups),
        ("ctx", "grp", "sub"),
    )
    heads = ("grp", "sub")
    return jax.shard_map(
        per_device,
        mesh=split,
        in_specs=(
            P("ctx", heads, None),
            P(None, "ctx", None),
            P(None, "ctx", None),
            P("ctx", heads, None),
            P("ctx", None, None),
            P("ctx", None, None),
        ),
        out_specs=(P("ctx", heads, None), P(None, "ctx", None), P(None, "ctx", None)),
        check_vma=False,
    )
```

```python
import functools

import jax
import jax.numpy as jnp
import numpy as np
from jax import lax
from jax.experimental import pallas as pl
from jax.experimental.pallas import tpu as pltpu
from jax.sharding import Mesh
from jax.sharding import PartitionSpec as P

HPG = 16
BLOCK = 64
REACH = 6


def cycled(value, axis, steps):
    count = lax.axis_size(axis)
    return lax.ppermute(value, axis, [(source, (source + steps) % count) for source in range(count)])


def chip_pairs(count, step):
    nearer = [(target - (2 * step - 1), target) for target in range(0, count, 2)]
    farther = [(target - (2 * step + 1), target) for target in range(1, count, 2)]
    return [(source, target) for source, target in nearer + farther if source >= 0]


def chip_fetch(value, axis, step):
    return lax.ppermute(value, axis, chip_pairs(lax.axis_size(axis), step))


def chip_return(value, axis, step):
    pairs = chip_pairs(lax.axis_size(axis), step)
    return lax.ppermute(value, axis, [(target, source) for source, target in pairs])


def swap_cores(value, axis):
    count = lax.axis_size(axis)
    return lax.ppermute(value, axis, [(source, source ^ 1) for source in range(count)])


def block_kernel(slots_ref, q_ref, do_ref, code_ref, k_ref, v_ref, dq_ref, dk_ref, dv_ref,
                 k_sel, v_sel, *, inv_root, heads_here):
    step = pl.program_id(0)
    slots = k_sel.shape[0] // BLOCK

    @pl.when(step == 0)
    def _():
        dk_ref[...] = jnp.zeros_like(dk_ref)
        dv_ref[...] = jnp.zeros_like(dv_ref)

    for slot in range(slots):
        start = pl.multiple_of(slots_ref[step, slot] * BLOCK, BLOCK)
        k_sel[slot * BLOCK:(slot + 1) * BLOCK, :] = k_ref[pl.ds(start, BLOCK), :]
        v_sel[slot * BLOCK:(slot + 1) * BLOCK, :] = v_ref[pl.ds(start, BLOCK), :]
    q = q_ref[...]
    do = do_ref[...]
    keys = k_sel[...]
    values = v_sel[...]
    rows, cols = q.shape[0], keys.shape[0]
    scores = lax.dot_general(
        q, keys, (((1,), (1,)), ((), ())), preferred_element_type=jnp.float32
    ) * inv_root
    query_pos = lax.broadcasted_iota(jnp.int32, (rows, 1), 0) // heads_here
    allowed = query_pos >= code_ref[...]
    scores = jnp.where(allowed, scores, -1e30)
    row_max = jnp.max(scores, axis=1, keepdims=True)
    shifted = jnp.exp(scores - row_max)
    weights = shifted * (1.0 / jnp.sum(shifted, axis=1, keepdims=True))
    weights_b = weights.astype(jnp.bfloat16)
    output = jnp.dot(weights_b, values, preferred_element_type=jnp.float32)
    row_delta = jnp.sum(do.astype(jnp.float32) * output, axis=1, keepdims=True)
    prob_grad = lax.dot_general(
        do, values, (((1,), (1,)), ((), ())), preferred_element_type=jnp.float32
    )
    score_b = (weights * (prob_grad - row_delta)).astype(jnp.bfloat16)
    query_part = jnp.dot(score_b, keys, preferred_element_type=jnp.float32) * inv_root
    dq_ref[...] = query_part.astype(jnp.bfloat16)
    key_part = lax.dot_general(
        score_b, q, (((0,), (0,)), ((), ())), preferred_element_type=jnp.float32
    ) * inv_root
    value_part = lax.dot_general(
        weights_b, do, (((0,), (0,)), ((), ())), preferred_element_type=jnp.float32
    )
    for slot in range(slots):
        start = pl.multiple_of(slots_ref[step, slot] * BLOCK, BLOCK)
        dk_ref[pl.ds(start, BLOCK), :] += key_part[slot * BLOCK:(slot + 1) * BLOCK]
        dv_ref[pl.ds(start, BLOCK), :] += value_part[slot * BLOCK:(slot + 1) * BLOCK]


def local_grads(queries, out_grad, key_tiles, value_tiles, slot_index, code, inv_root,
                interpret=False):
    tokens_here, heads_here, width = queries.shape
    blocks_here, slots = slot_index.shape
    rows = BLOCK * heads_here
    store = key_tiles.shape[0] * BLOCK
    cols = slots * BLOCK
    key_pos = jnp.tile(jnp.arange(BLOCK, dtype=jnp.int32), slots)[None, :]
    code_cols = jnp.repeat(code.astype(jnp.int32), BLOCK, axis=1)
    code_cols = jnp.where(code_cols == 2, 0, jnp.where(code_cols == 1, key_pos, BLOCK))
    code_cols = code_cols.reshape(blocks_here, 1, cols)
    kernel = functools.partial(block_kernel, inv_root=inv_root, heads_here=heads_here)
    whole = lambda step, slots_ref: (0, 0)
    per_block = lambda step, slots_ref: (step, 0)
    query_grad, key_grad, value_grad = pl.pallas_call(
        kernel,
        grid_spec=pltpu.PrefetchScalarGridSpec(
            num_scalar_prefetch=1,
            grid=(blocks_here,),
            in_specs=[
                pl.BlockSpec((rows, width), per_block),
                pl.BlockSpec((rows, width), per_block),
                pl.BlockSpec((None, 1, cols), lambda step, slots_ref: (step, 0, 0)),
                pl.BlockSpec((store, width), whole),
                pl.BlockSpec((store, width), whole),
            ],
            out_specs=[
                pl.BlockSpec((rows, width), per_block),
                pl.BlockSpec((store, width), whole),
                pl.BlockSpec((store, width), whole),
            ],
            scratch_shapes=[
                pltpu.VMEM((cols, width), jnp.bfloat16),
                pltpu.VMEM((cols, width), jnp.bfloat16),
            ],
        ),
        out_shape=[
            jax.ShapeDtypeStruct((tokens_here * heads_here, width), jnp.bfloat16),
            jax.ShapeDtypeStruct((store, width), jnp.float32),
            jax.ShapeDtypeStruct((store, width), jnp.float32),
        ],
        compiler_params=pltpu.CompilerParams(dimension_semantics=("arbitrary",)),
        interpret=interpret,
    )(
        slot_index.astype(jnp.int32),
        queries.reshape(tokens_here * heads_here, width),
        out_grad.reshape(tokens_here * heads_here, width),
        code_cols,
        key_tiles.reshape(store, width),
        value_tiles.reshape(store, width),
    )
    return query_grad.reshape(tokens_here, heads_here, width), key_grad, value_grad


def per_device(queries, key_rows, value_rows, out_grad, selected, live_slots):
    tokens_here, heads_here, width = queries.shape
    groups = key_rows.shape[0]
    blocks_here = tokens_here // BLOCK
    reach_span = REACH + 1
    inv_root = width ** (-0.5)
    ctx_index = lax.axis_index("ctx")
    group_index = lax.axis_index("grp")
    part_index = lax.axis_index("sub")
    parts_count = lax.axis_size("sub")
    quarter = tokens_here // parts_count
    own_tiles = jnp.stack(
        [
            lax.dynamic_index_in_dim(key_rows, group_index, 0, keepdims=False),
            lax.dynamic_index_in_dim(value_rows, group_index, 0, keepdims=False),
        ]
    )
    rolled = jnp.roll(own_tiles, -part_index * quarter, axis=1)
    own_part = rolled[:, :quarter]
    even = ctx_index % 2 == 0
    took = [chip_fetch(own_part, "ctx", step) for step in range(1, 4)]
    other = swap_cores(jnp.stack([own_part] + took), "ctx")
    fetched = jnp.stack(
        [
            jnp.where(even, took[0], other[0]),
            other[1],
            jnp.where(even, took[1], took[0]),
            other[2],
            jnp.where(even, took[2], took[1]),
            other[3],
        ]
    )
    pieces = [fetched] + [cycled(fetched, "sub", -step) for step in range(1, parts_count)]
    tile_store = jnp.concatenate([rolled[None], jnp.concatenate(pieces, axis=2)], axis=0)
    key_tiles = tile_store[:, 0].reshape(reach_span * blocks_here, BLOCK, width)
    value_tiles = tile_store[:, 1].reshape(reach_span * blocks_here, BLOCK, width)
    chosen = lax.dynamic_index_in_dim(selected, group_index, 1, keepdims=False)
    live_mask = lax.dynamic_index_in_dim(live_slots, group_index, 1, keepdims=False)
    block_ids = ctx_index * blocks_here + jnp.arange(blocks_here, dtype=jnp.int32)
    local_block = chosen % blocks_here
    per_part = blocks_here // parts_count
    rolled_block = (local_block // per_part - part_index) % parts_count * per_part + local_block % per_part
    slot_index = (ctx_index - chosen // blocks_here) * blocks_here + rolled_block
    slot_index = jnp.clip(slot_index, 0, reach_span * blocks_here - 1)
    code = jnp.where(live_mask == 1, jnp.where(chosen < block_ids[:, None], 2, 1), 0)
    query_grad, key_grad, value_grad = local_grads(
        queries, out_grad, key_tiles, value_tiles, slot_index, code, inv_root
    )
    grads = jnp.stack([key_grad, value_grad]).reshape(2, reach_span, tokens_here, width)
    sent = grads.astype(jnp.bfloat16)

    def reduce_parts(offsets):
        part = jnp.stack([grads[:, offset, :quarter] for offset in offsets], axis=1)
        for step in range(1, parts_count):
            piece = jnp.stack(
                [sent[:, offset, step * quarter:(step + 1) * quarter] for offset in offsets], axis=1
            )
            part = part + cycled(piece, "sub", step).astype(jnp.float32)
        return dict(zip(offsets, [part[:, index] for index in range(len(offsets))]))

    shared = reduce_parts((1, 2, 4, 6))
    other = swap_cores(
        jnp.stack([shared[1], shared[2], shared[4], shared[6]]).astype(jnp.bfloat16), "ctx"
    ).astype(jnp.float32)
    kept = reduce_parts((0, 3, 5))
    running = kept[0] + jnp.where(even, other[0], 0.0)
    outgoing = [
        jnp.where(even, shared[1] + other[1], kept[3] + other[1]),
        jnp.where(even, kept[3] + other[2], kept[5] + other[2]),
        jnp.where(even, kept[5] + other[3], other[3]),
    ]
    for step, term in enumerate(outgoing, start=1):
        running = running + chip_return(term.astype(jnp.bfloat16), "ctx", step).astype(jnp.float32)
    mine = running.astype(jnp.bfloat16)
    by_group = jnp.stack([mine] + [cycled(mine, "grp", -step) for step in range(1, groups)])
    by_part = jnp.stack([by_group] + [cycled(by_group, "sub", -step) for step in range(1, parts_count)])
    part_order = (jnp.arange(parts_count) - part_index) % parts_count
    group_order = (jnp.arange(groups) - group_index) % groups
    flat_order = (part_order[None, :] * groups + group_order[:, None]).reshape(-1)
    ordered = jnp.take(by_part.reshape((parts_count * groups,) + mine.shape), flat_order, axis=0)
    ordered = ordered.reshape((groups, parts_count) + mine.shape)
    summed = jnp.transpose(ordered, (2, 0, 1, 3, 4)).reshape(2, groups, tokens_here, width)
    summed = summed.astype(jnp.float32)
    return (query_grad, summed[0], summed[1])


def solution(mesh):
    ctx_count, head_count = mesh.devices.shape
    groups = 4
    split = Mesh(
        np.asarray(mesh.devices).reshape(ctx_count, groups, head_count // groups),
        ("ctx", "grp", "sub"),
    )
    heads = ("grp", "sub")
    return jax.shard_map(
        per_device,
        mesh=split,
        in_specs=(
            P("ctx", heads, None),
            P(None, "ctx", None),
            P(None, "ctx", None),
            P("ctx", heads, None),
            P("ctx", None, None),
            P("ctx", None, None),
        ),
        out_specs=(P("ctx", heads, None), P(None, "ctx", None), P(None, "ctx", None)),
        check_vma=False,
    )
```

```python
import functools

import jax
import jax.numpy as jnp
import numpy as np
from jax import lax
from jax.experimental import pallas as pl
from jax.experimental.pallas import tpu as pltpu
from jax.sharding import Mesh
from jax.sharding import PartitionSpec as P

HPG = 16
BLOCK = 64
REACH = 6


def cycled(value, axis, steps):
    count = lax.axis_size(axis)
    return lax.ppermute(value, axis, [(source, (source + steps) % count) for source in range(count)])


def chip_pairs(count, step):
    nearer = [(target - (2 * step - 1), target) for target in range(0, count, 2)]
    farther = [(target - (2 * step + 1), target) for target in range(1, count, 2)]
    return [(source, target) for source, target in nearer + farther if source >= 0]


def chip_fetch(value, axis, step):
    return lax.ppermute(value, axis, chip_pairs(lax.axis_size(axis), step))


def chip_return(value, axis, step):
    pairs = chip_pairs(lax.axis_size(axis), step)
    return lax.ppermute(value, axis, [(target, source) for source, target in pairs])


def swap_cores(value, axis):
    count = lax.axis_size(axis)
    return lax.ppermute(value, axis, [(source, source ^ 1) for source in range(count)])


def block_kernel(slots_ref, q_ref, do_ref, code_ref, k_ref, v_ref, dq_ref, dk_ref, dv_ref,
                 k_sel, v_sel, *, inv_root, heads_here):
    step = pl.program_id(0)
    slots = k_sel.shape[0] // BLOCK

    @pl.when(step == 0)
    def _():
        dk_ref[...] = jnp.zeros_like(dk_ref)
        dv_ref[...] = jnp.zeros_like(dv_ref)

    for slot in range(slots):
        start = pl.multiple_of(slots_ref[step, slot] * BLOCK, BLOCK)
        k_sel[slot * BLOCK:(slot + 1) * BLOCK, :] = k_ref[pl.ds(start, BLOCK), :]
        v_sel[slot * BLOCK:(slot + 1) * BLOCK, :] = v_ref[pl.ds(start, BLOCK), :]
    q = q_ref[...]
    do = do_ref[...]
    keys = k_sel[...]
    values = v_sel[...]
    rows, cols = q.shape[0], keys.shape[0]
    scores = lax.dot_general(
        q, keys, (((1,), (1,)), ((), ())), preferred_element_type=jnp.float32
    ) * inv_root
    query_pos = lax.broadcasted_iota(jnp.int32, (rows, 1), 0) // heads_here
    allowed = query_pos >= code_ref[...]
    scores = jnp.where(allowed, scores, -1e30)
    row_max = jnp.max(scores, axis=1, keepdims=True)
    shifted = jnp.exp(scores - row_max)
    weights = shifted * (1.0 / jnp.sum(shifted, axis=1, keepdims=True))
    weights_b = weights.astype(jnp.bfloat16)
    output = jnp.dot(weights_b, values, preferred_element_type=jnp.float32)
    row_delta = jnp.sum(do.astype(jnp.float32) * output, axis=1, keepdims=True)
    prob_grad = lax.dot_general(
        do, values, (((1,), (1,)), ((), ())), preferred_element_type=jnp.float32
    )
    score_b = (weights * (prob_grad - row_delta)).astype(jnp.bfloat16)
    query_part = jnp.dot(score_b, keys, preferred_element_type=jnp.float32) * inv_root
    dq_ref[...] = query_part.astype(jnp.bfloat16)
    key_part = lax.dot_general(
        score_b, q, (((0,), (0,)), ((), ())), preferred_element_type=jnp.float32
    ) * inv_root
    value_part = lax.dot_general(
        weights_b, do, (((0,), (0,)), ((), ())), preferred_element_type=jnp.float32
    )
    for slot in range(slots):
        start = pl.multiple_of(slots_ref[step, slot] * BLOCK, BLOCK)
        dk_ref[pl.ds(start, BLOCK), :] += key_part[slot * BLOCK:(slot + 1) * BLOCK]
        dv_ref[pl.ds(start, BLOCK), :] += value_part[slot * BLOCK:(slot + 1) * BLOCK]


def local_grads(queries, out_grad, key_tiles, value_tiles, slot_index, code, inv_root,
                interpret=False):
    tokens_here, heads_here, width = queries.shape
    blocks_here, slots = slot_index.shape
    rows = BLOCK * heads_here
    store = key_tiles.shape[0] * BLOCK
    cols = slots * BLOCK
    key_pos = jnp.tile(jnp.arange(BLOCK, dtype=jnp.int32), slots)[None, :]
    code_cols = jnp.repeat(code.astype(jnp.int32), BLOCK, axis=1)
    code_cols = jnp.where(code_cols == 2, 0, jnp.where(code_cols == 1, key_pos, BLOCK))
    code_cols = code_cols.reshape(blocks_here, 1, cols)
    kernel = functools.partial(block_kernel, inv_root=inv_root, heads_here=heads_here)
    whole = lambda step, slots_ref: (0, 0)
    per_block = lambda step, slots_ref: (step, 0)
    query_grad, key_grad, value_grad = pl.pallas_call(
        kernel,
        grid_spec=pltpu.PrefetchScalarGridSpec(
            num_scalar_prefetch=1,
            grid=(blocks_here,),
            in_specs=[
                pl.BlockSpec((rows, width), per_block),
                pl.BlockSpec((rows, width), per_block),
                pl.BlockSpec((None, 1, cols), lambda step, slots_ref: (step, 0, 0)),
                pl.BlockSpec((store, width), whole),
                pl.BlockSpec((store, width), whole),
            ],
            out_specs=[
                pl.BlockSpec((rows, width), per_block),
                pl.BlockSpec((store, width), whole),
                pl.BlockSpec((store, width), whole),
            ],
            scratch_shapes=[
                pltpu.VMEM((cols, width), jnp.bfloat16),
                pltpu.VMEM((cols, width), jnp.bfloat16),
            ],
        ),
        out_shape=[
            jax.ShapeDtypeStruct((tokens_here * heads_here, width), jnp.bfloat16),
            jax.ShapeDtypeStruct((store, width), jnp.float32),
            jax.ShapeDtypeStruct((store, width), jnp.float32),
        ],
        compiler_params=pltpu.CompilerParams(dimension_semantics=("arbitrary",)),
        interpret=interpret,
    )(
        slot_index.astype(jnp.int32),
        queries.reshape(tokens_here * heads_here, width),
        out_grad.reshape(tokens_here * heads_here, width),
        code_cols,
        key_tiles.reshape(store, width),
        value_tiles.reshape(store, width),
    )
    return query_grad.reshape(tokens_here, heads_here, width), key_grad, value_grad


def per_device(queries, key_rows, value_rows, out_grad, selected, live_slots):
    tokens_here, heads_here, width = queries.shape
    groups = key_rows.shape[0]
    blocks_here = tokens_here // BLOCK
    reach_span = REACH + 1
    inv_root = width ** (-0.5)
    ctx_index = lax.axis_index("ctx")
    group_index = lax.axis_index("grp")
    part_index = lax.axis_index("sub")
    parts_count = lax.axis_size("sub")
    quarter = tokens_here // parts_count
    own_tiles = jnp.stack(
        [
            lax.dynamic_index_in_dim(key_rows, group_index, 0, keepdims=False),
            lax.dynamic_index_in_dim(value_rows, group_index, 0, keepdims=False),
        ]
    )
    rolled = jnp.roll(own_tiles, -part_index * quarter, axis=1)
    own_part = rolled[:, :quarter]
    even = ctx_index % 2 == 0
    took = jnp.stack([chip_fetch(own_part, "ctx", step) for step in range(1, 4)])
    pieces = [took] + [cycled(took, "sub", -step) for step in range(1, parts_count)]
    took = jnp.concatenate(pieces, axis=2)
    mine = jnp.concatenate([rolled[None], took], axis=0)
    tile_store = jnp.concatenate([mine, swap_cores(mine, "ctx")], axis=0)
    store_span = tile_store.shape[0]
    key_tiles = tile_store[:, 0].reshape(store_span * blocks_here, BLOCK, width)
    value_tiles = tile_store[:, 1].reshape(store_span * blocks_here, BLOCK, width)
    chosen = lax.dynamic_index_in_dim(selected, group_index, 1, keepdims=False)
    live_mask = lax.dynamic_index_in_dim(live_slots, group_index, 1, keepdims=False)
    block_ids = ctx_index * blocks_here + jnp.arange(blocks_here, dtype=jnp.int32)
    local_block = chosen % blocks_here
    per_part = blocks_here // parts_count
    rolled_block = (local_block // per_part - part_index) % parts_count * per_part + local_block % per_part
    offset = jnp.clip(ctx_index - chosen // blocks_here, 0, REACH)
    placed = jnp.where(
        even, jnp.array([0, 1, 5, 2, 6, 3, 7], jnp.int32)[offset], jnp.array([0, 4, 5, 1, 6, 2, 7], jnp.int32)[offset]
    )
    slot_index = placed * blocks_here + rolled_block
    code = jnp.where(live_mask == 1, jnp.where(chosen < block_ids[:, None], 2, 1), 0)
    query_grad, key_grad, value_grad = local_grads(
        queries, out_grad, key_tiles, value_tiles, slot_index, code, inv_root
    )
    grads = jnp.stack([key_grad, value_grad]).reshape(2, store_span, tokens_here, width)
    half = store_span // 2
    back = swap_cores(grads[:, half:].astype(jnp.bfloat16), "ctx").astype(jnp.float32)
    totals = grads[:, :half] + back
    sent = totals.astype(jnp.bfloat16)

    def reduce_parts(lo, hi):
        part = totals[:, lo:hi, :quarter]
        for step in range(1, parts_count):
            piece = sent[:, lo:hi, step * quarter:(step + 1) * quarter]
            part = part + cycled(piece, "sub", step).astype(jnp.float32)
        return part

    fetched_parts = reduce_parts(1, half)
    running = reduce_parts(0, 1)[:, 0]
    for step in range(1, half):
        term = fetched_parts[:, step - 1].astype(jnp.bfloat16)
        running = running + chip_return(term, "ctx", step).astype(jnp.float32)
    mine = running.astype(jnp.bfloat16)
    by_group = jnp.stack([mine] + [cycled(mine, "grp", -step) for step in range(1, groups)])
    by_part = jnp.stack([by_group] + [cycled(by_group, "sub", -step) for step in range(1, parts_count)])
    part_order = (jnp.arange(parts_count) - part_index) % parts_count
    group_order = (jnp.arange(groups) - group_index) % groups
    flat_order = (part_order[None, :] * groups + group_order[:, None]).reshape(-1)
    ordered = jnp.take(by_part.reshape((parts_count * groups,) + mine.shape), flat_order, axis=0)
    ordered = ordered.reshape((groups, parts_count) + mine.shape)
    summed = jnp.transpose(ordered, (2, 0, 1, 3, 4)).reshape(2, groups, tokens_here, width)
    summed = summed.astype(jnp.float32)
    return (query_grad, summed[0], summed[1])


def solution(mesh):
    ctx_count, head_count = mesh.devices.shape
    groups = 4
    split = Mesh(
        np.asarray(mesh.devices).reshape(ctx_count, groups, head_count // groups),
        ("ctx", "grp", "sub"),
    )
    heads = ("grp", "sub")
    return jax.shard_map(
        per_device,
        mesh=split,
        in_specs=(
            P("ctx", heads, None),
            P(None, "ctx", None),
            P(None, "ctx", None),
            P("ctx", heads, None),
            P("ctx", None, None),
            P("ctx", None, None),
        ),
        out_specs=(P("ctx", heads, None), P(None, "ctx", None), P(None, "ctx", None)),
        check_vma=False,
    )
```

```python
import functools

import jax
import jax.numpy as jnp
import numpy as np
from jax import lax
from jax.experimental import pallas as pl
from jax.experimental.pallas import tpu as pltpu
from jax.sharding import Mesh
from jax.sharding import PartitionSpec as P

HPG = 16
BLOCK = 64
REACH = 6


def cycled(value, axis, steps):
    count = lax.axis_size(axis)
    return lax.ppermute(value, axis, [(source, (source + steps) % count) for source in range(count)])


def chip_pairs(count, step):
    nearer = [(target - (2 * step - 1), target) for target in range(0, count, 2)]
    farther = [(target - (2 * step + 1), target) for target in range(1, count, 2)]
    return [(source, target) for source, target in nearer + farther if source >= 0]


def chip_fetch(value, axis, step):
    return lax.ppermute(value, axis, chip_pairs(lax.axis_size(axis), step))


def chip_return(value, axis, step):
    pairs = chip_pairs(lax.axis_size(axis), step)
    return lax.ppermute(value, axis, [(target, source) for source, target in pairs])


def swap_cores(value, axis):
    count = lax.axis_size(axis)
    return lax.ppermute(value, axis, [(source, source ^ 1) for source in range(count)])


def block_kernel(slots_ref, q_ref, do_ref, code_ref, k_ref, v_ref, dq_ref, dk_ref, dv_ref,
                 k_sel, v_sel, *, inv_root, heads_here):
    step = pl.program_id(0)
    slots = k_sel.shape[0] // BLOCK

    @pl.when(step == 0)
    def _():
        dk_ref[...] = jnp.zeros_like(dk_ref)
        dv_ref[...] = jnp.zeros_like(dv_ref)

    for slot in range(slots):
        start = pl.multiple_of(slots_ref[step, slot] * BLOCK, BLOCK)
        k_sel[slot * BLOCK:(slot + 1) * BLOCK, :] = k_ref[pl.ds(start, BLOCK), :]
        v_sel[slot * BLOCK:(slot + 1) * BLOCK, :] = v_ref[pl.ds(start, BLOCK), :]
    q = q_ref[...]
    do = do_ref[...]
    keys = k_sel[...]
    values = v_sel[...]
    rows, cols = q.shape[0], keys.shape[0]
    scores = lax.dot_general(
        q, keys, (((1,), (1,)), ((), ())), preferred_element_type=jnp.float32
    ) * inv_root
    query_pos = lax.broadcasted_iota(jnp.int32, (rows, 1), 0) // heads_here
    allowed = query_pos >= code_ref[...]
    scores = jnp.where(allowed, scores, -1e30)
    row_max = jnp.max(scores, axis=1, keepdims=True)
    shifted = jnp.exp(scores - row_max)
    weights = shifted * (1.0 / jnp.sum(shifted, axis=1, keepdims=True))
    weights_b = weights.astype(jnp.bfloat16)
    output = jnp.dot(weights_b, values, preferred_element_type=jnp.float32)
    row_delta = jnp.sum(do.astype(jnp.float32) * output, axis=1, keepdims=True)
    prob_grad = lax.dot_general(
        do, values, (((1,), (1,)), ((), ())), preferred_element_type=jnp.float32
    )
    score_b = (weights * (prob_grad - row_delta)).astype(jnp.bfloat16)
    query_part = jnp.dot(score_b, keys, preferred_element_type=jnp.float32) * inv_root
    dq_ref[...] = query_part.astype(jnp.bfloat16)
    key_part = lax.dot_general(
        score_b, q, (((0,), (0,)), ((), ())), preferred_element_type=jnp.float32
    ) * inv_root
    value_part = lax.dot_general(
        weights_b, do, (((0,), (0,)), ((), ())), preferred_element_type=jnp.float32
    )
    for slot in range(slots):
        start = pl.multiple_of(slots_ref[step, slot] * BLOCK, BLOCK)
        dk_ref[pl.ds(start, BLOCK), :] += key_part[slot * BLOCK:(slot + 1) * BLOCK]
        dv_ref[pl.ds(start, BLOCK), :] += value_part[slot * BLOCK:(slot + 1) * BLOCK]


def local_grads(queries, out_grad, key_tiles, value_tiles, slot_index, code, inv_root,
                interpret=False):
    tokens_here, heads_here, width = queries.shape
    blocks_here, slots = slot_index.shape
    rows = BLOCK * heads_here
    store = key_tiles.shape[0] * BLOCK
    cols = slots * BLOCK
    key_pos = jnp.tile(jnp.arange(BLOCK, dtype=jnp.int32), slots)[None, :]
    code_cols = jnp.repeat(code.astype(jnp.int32), BLOCK, axis=1)
    code_cols = jnp.where(code_cols == 2, 0, jnp.where(code_cols == 1, key_pos, BLOCK))
    code_cols = code_cols.reshape(blocks_here, 1, cols)
    kernel = functools.partial(block_kernel, inv_root=inv_root, heads_here=heads_here)
    whole = lambda step, slots_ref: (0, 0)
    per_block = lambda step, slots_ref: (step, 0)
    query_grad, key_grad, value_grad = pl.pallas_call(
        kernel,
        grid_spec=pltpu.PrefetchScalarGridSpec(
            num_scalar_prefetch=1,
            grid=(blocks_here,),
            in_specs=[
                pl.BlockSpec((rows, width), per_block),
                pl.BlockSpec((rows, width), per_block),
                pl.BlockSpec((None, 1, cols), lambda step, slots_ref: (step, 0, 0)),
                pl.BlockSpec((store, width), whole),
                pl.BlockSpec((store, width), whole),
            ],
            out_specs=[
                pl.BlockSpec((rows, width), per_block),
                pl.BlockSpec((store, width), whole),
                pl.BlockSpec((store, width), whole),
            ],
            scratch_shapes=[
                pltpu.VMEM((cols, width), jnp.bfloat16),
                pltpu.VMEM((cols, width), jnp.bfloat16),
            ],
        ),
        out_shape=[
            jax.ShapeDtypeStruct((tokens_here * heads_here, width), jnp.bfloat16),
            jax.ShapeDtypeStruct((store, width), jnp.float32),
            jax.ShapeDtypeStruct((store, width), jnp.float32),
        ],
        compiler_params=pltpu.CompilerParams(dimension_semantics=("arbitrary",)),
        interpret=interpret,
    )(
        slot_index.astype(jnp.int32),
        queries.reshape(tokens_here * heads_here, width),
        out_grad.reshape(tokens_here * heads_here, width),
        code_cols,
        key_tiles.reshape(store, width),
        value_tiles.reshape(store, width),
    )
    return query_grad.reshape(tokens_here, heads_here, width), key_grad, value_grad


def per_device(queries, key_rows, value_rows, out_grad, selected, live_slots):
    tokens_here, heads_here, width = queries.shape
    groups = key_rows.shape[0]
    blocks_here = tokens_here // BLOCK
    reach_span = REACH + 1
    inv_root = width ** (-0.5)
    ctx_index = lax.axis_index("ctx")
    group_index = lax.axis_index("grp")
    part_index = lax.axis_index("sub")
    parts_count = lax.axis_size("sub")
    quarter = tokens_here // parts_count
    own_tiles = jnp.stack(
        [
            lax.dynamic_index_in_dim(key_rows, group_index, 0, keepdims=False),
            lax.dynamic_index_in_dim(value_rows, group_index, 0, keepdims=False),
        ]
    )
    rolled = jnp.roll(own_tiles, -part_index * quarter, axis=1)
    own_part = rolled[:, :quarter]
    even = ctx_index % 2 == 0
    took = jnp.stack([chip_fetch(own_part, "ctx", step) for step in range(1, 4)])
    pieces = [took] + [cycled(took, "sub", -step) for step in range(1, parts_count)]
    took = jnp.concatenate(pieces, axis=2)
    mine = jnp.concatenate([rolled[None], took], axis=0)
    tile_store = jnp.concatenate([mine, swap_cores(mine, "ctx")], axis=0)
    store_span = tile_store.shape[0]
    key_tiles = tile_store[:, 0].reshape(store_span * blocks_here, BLOCK, width)
    value_tiles = tile_store[:, 1].reshape(store_span * blocks_here, BLOCK, width)
    chosen = lax.dynamic_index_in_dim(selected, group_index, 1, keepdims=False)
    live_mask = lax.dynamic_index_in_dim(live_slots, group_index, 1, keepdims=False)
    block_ids = ctx_index * blocks_here + jnp.arange(blocks_here, dtype=jnp.int32)
    local_block = chosen % blocks_here
    per_part = blocks_here // parts_count
    rolled_block = (local_block // per_part - part_index) % parts_count * per_part + local_block % per_part
    offset = jnp.clip(ctx_index - chosen // blocks_here, 0, REACH)
    placed = jnp.where(
        even, jnp.array([0, 1, 5, 2, 6, 3, 7], jnp.int32)[offset], jnp.array([0, 4, 5, 1, 6, 2, 7], jnp.int32)[offset]
    )
    slot_index = placed * blocks_here + rolled_block
    code = jnp.where(live_mask == 1, jnp.where(chosen < block_ids[:, None], 2, 1), 0)
    query_grad, key_grad, value_grad = local_grads(
        queries, out_grad, key_tiles, value_tiles, slot_index, code, inv_root
    )
    grads = jnp.stack([key_grad, value_grad]).reshape(2, store_span, tokens_here, width)
    half = store_span // 2
    back = swap_cores(grads[:, half:].astype(jnp.bfloat16), "ctx").astype(jnp.float32)
    totals = grads[:, :half] + back
    sent = totals.astype(jnp.bfloat16)

    def reduce_parts(lo, hi):
        part = totals[:, lo:hi, :quarter]
        for step in range(1, parts_count):
            piece = sent[:, lo:hi, step * quarter:(step + 1) * quarter]
            part = part + cycled(piece, "sub", step).astype(jnp.float32)
        return part

    reduced = reduce_parts(0, half)
    running = reduced[:, 0]
    for step in range(1, half):
        term = reduced[:, step].astype(jnp.bfloat16)
        running = running + chip_return(term, "ctx", step).astype(jnp.float32)
    mine = running.astype(jnp.bfloat16)
    by_group = jnp.stack([mine] + [cycled(mine, "grp", -step) for step in range(1, groups)])
    by_part = jnp.stack([by_group] + [cycled(by_group, "sub", -step) for step in range(1, parts_count)])
    part_order = (jnp.arange(parts_count) - part_index) % parts_count
    group_order = (jnp.arange(groups) - group_index) % groups
    flat_order = (part_order[None, :] * groups + group_order[:, None]).reshape(-1)
    ordered = jnp.take(by_part.reshape((parts_count * groups,) + mine.shape), flat_order, axis=0)
    ordered = ordered.reshape((groups, parts_count) + mine.shape)
    summed = jnp.transpose(ordered, (2, 0, 1, 3, 4)).reshape(2, groups, tokens_here, width)
    summed = summed.astype(jnp.float32)
    return (query_grad, summed[0], summed[1])


def solution(mesh):
    ctx_count, head_count = mesh.devices.shape
    groups = 4
    split = Mesh(
        np.asarray(mesh.devices).reshape(ctx_count, groups, head_count // groups),
        ("ctx", "grp", "sub"),
    )
    heads = ("grp", "sub")
    return jax.shard_map(
        per_device,
        mesh=split,
        in_specs=(
            P("ctx", heads, None),
            P(None, "ctx", None),
            P(None, "ctx", None),
            P("ctx", heads, None),
            P("ctx", None, None),
            P("ctx", None, None),
        ),
        out_specs=(P("ctx", heads, None), P(None, "ctx", None), P(None, "ctx", None)),
        check_vma=False,
    )
```

```python
import functools

import jax
import jax.numpy as jnp
import numpy as np
from jax import lax
from jax.experimental import pallas as pl
from jax.experimental.pallas import tpu as pltpu
from jax.sharding import Mesh
from jax.sharding import PartitionSpec as P

HPG = 16
BLOCK = 64
REACH = 6


def cycled(value, axis, steps):
    count = lax.axis_size(axis)
    return lax.ppermute(value, axis, [(source, (source + steps) % count) for source in range(count)])


def chip_pairs(count, step):
    nearer = [(target - (2 * step - 1), target) for target in range(0, count, 2)]
    farther = [(target - (2 * step + 1), target) for target in range(1, count, 2)]
    return [(source, target) for source, target in nearer + farther if source >= 0]


def chip_fetch(value, axis, step):
    return lax.ppermute(value, axis, chip_pairs(lax.axis_size(axis), step))


def chip_return(value, axis, step):
    pairs = chip_pairs(lax.axis_size(axis), step)
    return lax.ppermute(value, axis, [(target, source) for source, target in pairs])


def swap_cores(value, axis):
    count = lax.axis_size(axis)
    return lax.ppermute(value, axis, [(source, source ^ 1) for source in range(count)])


def block_kernel(slots_ref, q_ref, do_ref, code_ref, k_ref, v_ref, dq_ref, dk_ref, dv_ref,
                 k_sel, v_sel, *, inv_root, heads_here):
    step = pl.program_id(0)
    slots = k_sel.shape[0] // BLOCK

    @pl.when(step == 0)
    def _():
        dk_ref[...] = jnp.zeros_like(dk_ref)
        dv_ref[...] = jnp.zeros_like(dv_ref)

    for slot in range(slots):
        start = pl.multiple_of(slots_ref[step, slot] * BLOCK, BLOCK)
        k_sel[slot * BLOCK:(slot + 1) * BLOCK, :] = k_ref[pl.ds(start, BLOCK), :]
        v_sel[slot * BLOCK:(slot + 1) * BLOCK, :] = v_ref[pl.ds(start, BLOCK), :]
    q = q_ref[...]
    do = do_ref[...]
    keys = k_sel[...]
    values = v_sel[...]
    rows, cols = q.shape[0], keys.shape[0]
    scores = lax.dot_general(
        q, keys, (((1,), (1,)), ((), ())), preferred_element_type=jnp.float32
    ) * inv_root
    query_pos = lax.broadcasted_iota(jnp.int32, (rows, 1), 0) // heads_here
    allowed = query_pos >= code_ref[...]
    scores = jnp.where(allowed, scores, -1e30)
    row_max = jnp.max(scores, axis=1, keepdims=True)
    shifted = jnp.exp(scores - row_max)
    weights = shifted * (1.0 / jnp.sum(shifted, axis=1, keepdims=True))
    weights_b = weights.astype(jnp.bfloat16)
    output = jnp.dot(weights_b, values, preferred_element_type=jnp.float32)
    row_delta = jnp.sum(do.astype(jnp.float32) * output, axis=1, keepdims=True)
    prob_grad = lax.dot_general(
        do, values, (((1,), (1,)), ((), ())), preferred_element_type=jnp.float32
    )
    score_b = (weights * (prob_grad - row_delta)).astype(jnp.bfloat16)
    query_part = jnp.dot(score_b, keys, preferred_element_type=jnp.float32) * inv_root
    dq_ref[...] = query_part.astype(jnp.bfloat16)
    key_part = lax.dot_general(
        score_b, q, (((0,), (0,)), ((), ())), preferred_element_type=jnp.float32
    ) * inv_root
    value_part = lax.dot_general(
        weights_b, do, (((0,), (0,)), ((), ())), preferred_element_type=jnp.float32
    )
    for slot in range(slots):
        start = pl.multiple_of(slots_ref[step, slot] * BLOCK, BLOCK)
        dk_ref[pl.ds(start, BLOCK), :] += key_part[slot * BLOCK:(slot + 1) * BLOCK]
        dv_ref[pl.ds(start, BLOCK), :] += value_part[slot * BLOCK:(slot + 1) * BLOCK]


def local_grads(queries, out_grad, key_tiles, value_tiles, slot_index, code, inv_root,
                interpret=False):
    tokens_here, heads_here, width = queries.shape
    blocks_here, slots = slot_index.shape
    rows = BLOCK * heads_here
    store = key_tiles.shape[0] * BLOCK
    cols = slots * BLOCK
    key_pos = jnp.tile(jnp.arange(BLOCK, dtype=jnp.int32), slots)[None, :]
    code_cols = jnp.repeat(code.astype(jnp.int32), BLOCK, axis=1)
    code_cols = jnp.where(code_cols == 2, 0, jnp.where(code_cols == 1, key_pos, BLOCK))
    code_cols = code_cols.reshape(blocks_here, 1, cols)
    kernel = functools.partial(block_kernel, inv_root=inv_root, heads_here=heads_here)
    whole = lambda step, slots_ref: (0, 0)
    per_block = lambda step, slots_ref: (step, 0)
    query_grad, key_grad, value_grad = pl.pallas_call(
        kernel,
        grid_spec=pltpu.PrefetchScalarGridSpec(
            num_scalar_prefetch=1,
            grid=(blocks_here,),
            in_specs=[
                pl.BlockSpec((rows, width), per_block),
                pl.BlockSpec((rows, width), per_block),
                pl.BlockSpec((None, 1, cols), lambda step, slots_ref: (step, 0, 0)),
                pl.BlockSpec((store, width), whole),
                pl.BlockSpec((store, width), whole),
            ],
            out_specs=[
                pl.BlockSpec((rows, width), per_block),
                pl.BlockSpec((store, width), whole),
                pl.BlockSpec((store, width), whole),
            ],
            scratch_shapes=[
                pltpu.VMEM((cols, width), jnp.bfloat16),
                pltpu.VMEM((cols, width), jnp.bfloat16),
            ],
        ),
        out_shape=[
            jax.ShapeDtypeStruct((tokens_here * heads_here, width), jnp.bfloat16),
            jax.ShapeDtypeStruct((store, width), jnp.float32),
            jax.ShapeDtypeStruct((store, width), jnp.float32),
        ],
        compiler_params=pltpu.CompilerParams(dimension_semantics=("arbitrary",)),
        interpret=interpret,
    )(
        slot_index.astype(jnp.int32),
        queries.reshape(tokens_here * heads_here, width),
        out_grad.reshape(tokens_here * heads_here, width),
        code_cols,
        key_tiles.reshape(store, width),
        value_tiles.reshape(store, width),
    )
    return query_grad.reshape(tokens_here, heads_here, width), key_grad, value_grad


def per_device(queries, key_rows, value_rows, out_grad, selected, live_slots):
    tokens_here, heads_here, width = queries.shape
    groups = key_rows.shape[0]
    blocks_here = tokens_here // BLOCK
    reach_span = REACH + 1
    inv_root = width ** (-0.5)
    ctx_index = lax.axis_index("ctx")
    group_index = lax.axis_index("grp")
    part_index = lax.axis_index("sub")
    parts_count = lax.axis_size("sub")
    quarter = tokens_here // parts_count
    own_tiles = jnp.stack(
        [
            lax.dynamic_index_in_dim(key_rows, group_index, 0, keepdims=False),
            lax.dynamic_index_in_dim(value_rows, group_index, 0, keepdims=False),
        ]
    )
    rolled = jnp.roll(own_tiles, -part_index * quarter, axis=1)
    own_part = rolled[:, :quarter]
    even = ctx_index % 2 == 0
    took = [chip_fetch(own_part, "ctx", 1)]
    for step in range(2, 4):
        took.append(chip_fetch(took[-1], "ctx", 1))
    took = jnp.stack(took)
    pieces = [took] + [cycled(took, "sub", -step) for step in range(1, parts_count)]
    took = jnp.concatenate(pieces, axis=2)
    mine = jnp.concatenate([rolled[None], took], axis=0)
    tile_store = jnp.concatenate([mine, swap_cores(mine, "ctx")], axis=0)
    store_span = tile_store.shape[0]
    key_tiles = tile_store[:, 0].reshape(store_span * blocks_here, BLOCK, width)
    value_tiles = tile_store[:, 1].reshape(store_span * blocks_here, BLOCK, width)
    chosen = lax.dynamic_index_in_dim(selected, group_index, 1, keepdims=False)
    live_mask = lax.dynamic_index_in_dim(live_slots, group_index, 1, keepdims=False)
    block_ids = ctx_index * blocks_here + jnp.arange(blocks_here, dtype=jnp.int32)
    local_block = chosen % blocks_here
    per_part = blocks_here // parts_count
    rolled_block = (local_block // per_part - part_index) % parts_count * per_part + local_block % per_part
    offset = jnp.clip(ctx_index - chosen // blocks_here, 0, REACH)
    placed = jnp.where(
        even, jnp.array([0, 1, 5, 6, 2, 3, 7], jnp.int32)[offset], jnp.array([0, 4, 5, 1, 2, 6, 7], jnp.int32)[offset]
    )
    slot_index = placed * blocks_here + rolled_block
    code = jnp.where(live_mask == 1, jnp.where(chosen < block_ids[:, None], 2, 1), 0)
    query_grad, key_grad, value_grad = local_grads(
        queries, out_grad, key_tiles, value_tiles, slot_index, code, inv_root
    )
    grads = jnp.stack([key_grad, value_grad]).reshape(2, store_span, tokens_here, width)
    half = store_span // 2
    back = swap_cores(grads[:, half:].astype(jnp.bfloat16), "ctx").astype(jnp.float32)
    totals = grads[:, :half] + back
    sent = totals.astype(jnp.bfloat16)

    def reduce_parts(lo, hi):
        part = totals[:, lo:hi, :quarter]
        for step in range(1, parts_count):
            piece = sent[:, lo:hi, step * quarter:(step + 1) * quarter]
            part = part + cycled(piece, "sub", step).astype(jnp.float32)
        return part

    reduced = reduce_parts(0, half)
    running = reduced[:, half - 1]
    for step in range(half - 2, -1, -1):
        returned = chip_return(running.astype(jnp.bfloat16), "ctx", 1)
        running = reduced[:, step] + returned.astype(jnp.float32)
    mine = running.astype(jnp.bfloat16)
    by_group = jnp.stack([mine] + [cycled(mine, "grp", -step) for step in range(1, groups)])
    by_part = jnp.stack([by_group] + [cycled(by_group, "sub", -step) for step in range(1, parts_count)])
    part_order = (jnp.arange(parts_count) - part_index) % parts_count
    group_order = (jnp.arange(groups) - group_index) % groups
    flat_order = (part_order[None, :] * groups + group_order[:, None]).reshape(-1)
    ordered = jnp.take(by_part.reshape((parts_count * groups,) + mine.shape), flat_order, axis=0)
    ordered = ordered.reshape((groups, parts_count) + mine.shape)
    summed = jnp.transpose(ordered, (2, 0, 1, 3, 4)).reshape(2, groups, tokens_here, width)
    summed = summed.astype(jnp.float32)
    return (query_grad, summed[0], summed[1])


def solution(mesh):
    ctx_count, head_count = mesh.devices.shape
    groups = 4
    split = Mesh(
        np.asarray(mesh.devices).reshape(ctx_count, groups, head_count // groups),
        ("ctx", "grp", "sub"),
    )
    heads = ("grp", "sub")
    return jax.shard_map(
        per_device,
        mesh=split,
        in_specs=(
            P("ctx", heads, None),
            P(None, "ctx", None),
            P(None, "ctx", None),
            P("ctx", heads, None),
            P("ctx", None, None),
            P("ctx", None, None),
        ),
        out_specs=(P("ctx", heads, None), P(None, "ctx", None), P(None, "ctx", None)),
        check_vma=False,
    )
```

```python
import functools

import jax
import jax.numpy as jnp
import numpy as np
from jax import lax
from jax.experimental import pallas as pl
from jax.experimental.pallas import tpu as pltpu
from jax.sharding import Mesh
from jax.sharding import PartitionSpec as P

HPG = 16
BLOCK = 64
REACH = 6


def cycled(value, axis, steps):
    count = lax.axis_size(axis)
    return lax.ppermute(value, axis, [(source, (source + steps) % count) for source in range(count)])


def chip_pairs(count, step):
    nearer = [(target - (2 * step - 1), target) for target in range(0, count, 2)]
    farther = [(target - (2 * step + 1), target) for target in range(1, count, 2)]
    return [(source, target) for source, target in nearer + farther if source >= 0]


def chip_fetch(value, axis, step):
    return lax.ppermute(value, axis, chip_pairs(lax.axis_size(axis), step))


def chip_return(value, axis, step):
    pairs = chip_pairs(lax.axis_size(axis), step)
    return lax.ppermute(value, axis, [(target, source) for source, target in pairs])


def swap_cores(value, axis):
    count = lax.axis_size(axis)
    return lax.ppermute(value, axis, [(source, source ^ 1) for source in range(count)])


def block_kernel(slots_ref, q_ref, do_ref, code_ref, near_ref, far_ref, dq_ref, dkv_ref,
                 k_sel, v_sel, *, inv_root, heads_here):
    step = pl.program_id(0)
    slots = k_sel.shape[0] // BLOCK
    half, per_tile = near_ref.shape[0], near_ref.shape[2] // BLOCK

    @pl.when(step == 0)
    def _():
        dkv_ref[...] = jnp.zeros_like(dkv_ref)

    for slot in range(slots):
        tile = slots_ref[step, slot] // per_tile
        row = pl.multiple_of(slots_ref[step, slot] % per_tile * BLOCK, BLOCK)
        target = slice(slot * BLOCK, (slot + 1) * BLOCK)

        @pl.when(tile < half)
        def _():
            here = jnp.minimum(tile, half - 1)
            k_sel[target, :] = near_ref[here, 0, pl.ds(row, BLOCK), :]
            v_sel[target, :] = near_ref[here, 1, pl.ds(row, BLOCK), :]

        @pl.when(tile >= half)
        def _():
            there = jnp.maximum(tile - half, 0)
            k_sel[target, :] = far_ref[there, 0, pl.ds(row, BLOCK), :]
            v_sel[target, :] = far_ref[there, 1, pl.ds(row, BLOCK), :]
    q = q_ref[...]
    do = do_ref[...]
    keys = k_sel[...]
    values = v_sel[...]
    rows, cols = q.shape[0], keys.shape[0]
    scores = lax.dot_general(
        q, keys, (((1,), (1,)), ((), ())), preferred_element_type=jnp.float32
    ) * inv_root
    query_pos = lax.broadcasted_iota(jnp.int32, (rows, 1), 0) // heads_here
    allowed = query_pos >= code_ref[...]
    scores = jnp.where(allowed, scores, -1e30)
    row_max = jnp.max(scores, axis=1, keepdims=True)
    shifted = jnp.exp(scores - row_max)
    weights = shifted * (1.0 / jnp.sum(shifted, axis=1, keepdims=True))
    weights_b = weights.astype(jnp.bfloat16)
    output = jnp.dot(weights_b, values, preferred_element_type=jnp.float32)
    row_delta = jnp.sum(do.astype(jnp.float32) * output, axis=1, keepdims=True)
    prob_grad = lax.dot_general(
        do, values, (((1,), (1,)), ((), ())), preferred_element_type=jnp.float32
    )
    score_b = (weights * (prob_grad - row_delta)).astype(jnp.bfloat16)
    query_part = jnp.dot(score_b, keys, preferred_element_type=jnp.float32) * inv_root
    dq_ref[...] = query_part.astype(jnp.bfloat16)
    key_part = lax.dot_general(
        score_b, q, (((0,), (0,)), ((), ())), preferred_element_type=jnp.float32
    ) * inv_root
    value_part = lax.dot_general(
        weights_b, do, (((0,), (0,)), ((), ())), preferred_element_type=jnp.float32
    )
    for slot in range(slots):
        start = pl.multiple_of(slots_ref[step, slot] * BLOCK, BLOCK)
        dkv_ref[0, pl.ds(start, BLOCK), :] += key_part[slot * BLOCK:(slot + 1) * BLOCK]
        dkv_ref[1, pl.ds(start, BLOCK), :] += value_part[slot * BLOCK:(slot + 1) * BLOCK]


def local_grads(queries, out_grad, near, far, slot_index, code, inv_root, interpret=False):
    tokens_here, heads_here, width = queries.shape
    blocks_here, slots = slot_index.shape
    rows = BLOCK * heads_here
    store = (near.shape[0] + far.shape[0]) * near.shape[2]
    cols = slots * BLOCK
    key_pos = jnp.tile(jnp.arange(BLOCK, dtype=jnp.int32), slots)[None, :]
    code_cols = jnp.repeat(code.astype(jnp.int32), BLOCK, axis=1)
    code_cols = jnp.where(code_cols == 2, 0, jnp.where(code_cols == 1, key_pos, BLOCK))
    code_cols = code_cols.reshape(blocks_here, 1, cols)
    kernel = functools.partial(block_kernel, inv_root=inv_root, heads_here=heads_here)
    whole = lambda step, slots_ref: (0, 0)
    per_block = lambda step, slots_ref: (step, 0)
    query_grad, grads = pl.pallas_call(
        kernel,
        grid_spec=pltpu.PrefetchScalarGridSpec(
            num_scalar_prefetch=1,
            grid=(blocks_here,),
            in_specs=[
                pl.BlockSpec((rows, width), per_block),
                pl.BlockSpec((rows, width), per_block),
                pl.BlockSpec((None, 1, cols), lambda step, slots_ref: (step, 0, 0)),
                pl.BlockSpec(near.shape, lambda step, slots_ref: (0, 0, 0, 0)),
                pl.BlockSpec(far.shape, lambda step, slots_ref: (0, 0, 0, 0)),
            ],
            out_specs=[
                pl.BlockSpec((rows, width), per_block),
                pl.BlockSpec((2, store, width), lambda step, slots_ref: (0, 0, 0)),
            ],
            scratch_shapes=[
                pltpu.VMEM((cols, width), jnp.bfloat16),
                pltpu.VMEM((cols, width), jnp.bfloat16),
            ],
        ),
        out_shape=[
            jax.ShapeDtypeStruct((tokens_here * heads_here, width), jnp.bfloat16),
            jax.ShapeDtypeStruct((2, store, width), jnp.float32),
        ],
        compiler_params=pltpu.CompilerParams(dimension_semantics=("arbitrary",)),
        interpret=interpret,
    )(
        slot_index.astype(jnp.int32),
        queries.reshape(tokens_here * heads_here, width),
        out_grad.reshape(tokens_here * heads_here, width),
        code_cols,
        near,
        far,
    )
    return query_grad.reshape(tokens_here, heads_here, width), grads


def per_device(queries, key_rows, value_rows, out_grad, selected, live_slots):
    tokens_here, heads_here, width = queries.shape
    groups = key_rows.shape[0]
    blocks_here = tokens_here // BLOCK
    reach_span = REACH + 1
    inv_root = width ** (-0.5)
    ctx_index = lax.axis_index("ctx")
    group_index = lax.axis_index("grp")
    part_index = lax.axis_index("sub")
    parts_count = lax.axis_size("sub")
    quarter = tokens_here // parts_count
    own_tiles = jnp.stack(
        [
            lax.dynamic_index_in_dim(key_rows, group_index, 0, keepdims=False),
            lax.dynamic_index_in_dim(value_rows, group_index, 0, keepdims=False),
        ]
    )
    rolled = jnp.roll(own_tiles, -part_index * quarter, axis=1)
    own_part = rolled[:, :quarter]
    even = ctx_index % 2 == 0
    took = jnp.stack([chip_fetch(own_part, "ctx", step) for step in range(1, 4)])
    pieces = [took] + [cycled(took, "sub", -step) for step in range(1, parts_count)]
    took = jnp.concatenate(pieces, axis=2)
    mine = jnp.concatenate([rolled[None], took], axis=0)
    partner_tiles = swap_cores(mine, "ctx")
    store_span = 2 * mine.shape[0]
    chosen = lax.dynamic_index_in_dim(selected, group_index, 1, keepdims=False)
    live_mask = lax.dynamic_index_in_dim(live_slots, group_index, 1, keepdims=False)
    block_ids = ctx_index * blocks_here + jnp.arange(blocks_here, dtype=jnp.int32)
    local_block = chosen % blocks_here
    per_part = blocks_here // parts_count
    rolled_block = (local_block // per_part - part_index) % parts_count * per_part + local_block % per_part
    offset = jnp.clip(ctx_index - chosen // blocks_here, 0, REACH)
    placed = jnp.where(
        even, jnp.array([0, 1, 5, 2, 6, 3, 7], jnp.int32)[offset], jnp.array([0, 4, 5, 1, 6, 2, 7], jnp.int32)[offset]
    )
    slot_index = placed * blocks_here + rolled_block
    code = jnp.where(live_mask == 1, jnp.where(chosen < block_ids[:, None], 2, 1), 0)
    query_grad, grads = local_grads(
        queries, out_grad, mine, partner_tiles, slot_index, code, inv_root
    )
    grads = grads.reshape(2, store_span, tokens_here, width)
    half = store_span // 2
    back = swap_cores(grads[:, half:].astype(jnp.bfloat16), "ctx").astype(jnp.float32)
    totals = grads[:, :half] + back
    sent = totals.astype(jnp.bfloat16)

    def reduce_parts(lo, hi):
        part = totals[:, lo:hi, :quarter]
        for step in range(1, parts_count):
            piece = sent[:, lo:hi, step * quarter:(step + 1) * quarter]
            part = part + cycled(piece, "sub", step).astype(jnp.float32)
        return part

    reduced = reduce_parts(0, half)
    running = reduced[:, 0]
    for step in range(1, half):
        term = reduced[:, step].astype(jnp.bfloat16)
        running = running + chip_return(term, "ctx", step).astype(jnp.float32)
    mine = running.astype(jnp.bfloat16)
    by_group = jnp.stack([mine] + [cycled(mine, "grp", -step) for step in range(1, groups)])
    by_part = jnp.stack([by_group] + [cycled(by_group, "sub", -step) for step in range(1, parts_count)])
    part_order = (jnp.arange(parts_count) - part_index) % parts_count
    group_order = (jnp.arange(groups) - group_index) % groups
    flat_order = (part_order[None, :] * groups + group_order[:, None]).reshape(-1)
    ordered = jnp.take(by_part.reshape((parts_count * groups,) + mine.shape), flat_order, axis=0)
    ordered = ordered.reshape((groups, parts_count) + mine.shape)
    summed = jnp.transpose(ordered, (2, 0, 1, 3, 4)).reshape(2, groups, tokens_here, width)
    summed = summed.astype(jnp.float32)
    return (query_grad, summed[0], summed[1])


def solution(mesh):
    ctx_count, head_count = mesh.devices.shape
    groups = 4
    split = Mesh(
        np.asarray(mesh.devices).reshape(ctx_count, groups, head_count // groups),
        ("ctx", "grp", "sub"),
    )
    heads = ("grp", "sub")
    return jax.shard_map(
        per_device,
        mesh=split,
        in_specs=(
            P("ctx", heads, None),
            P(None, "ctx", None),
            P(None, "ctx", None),
            P("ctx", heads, None),
            P("ctx", None, None),
            P("ctx", None, None),
        ),
        out_specs=(P("ctx", heads, None), P(None, "ctx", None), P(None, "ctx", None)),
        check_vma=False,
    )
```

```python
import functools

import jax
import jax.numpy as jnp
import numpy as np
from jax import lax
from jax.experimental import pallas as pl
from jax.experimental.pallas import tpu as pltpu
from jax.sharding import Mesh
from jax.sharding import PartitionSpec as P

HPG = 16
BLOCK = 64
REACH = 6


def cycled(value, axis, steps):
    count = lax.axis_size(axis)
    return lax.ppermute(value, axis, [(source, (source + steps) % count) for source in range(count)])


def chip_pairs(count, step):
    nearer = [(target - (2 * step - 1), target) for target in range(0, count, 2)]
    farther = [(target - (2 * step + 1), target) for target in range(1, count, 2)]
    return [(source, target) for source, target in nearer + farther if source >= 0]


def chip_fetch(value, axis, step):
    return lax.ppermute(value, axis, chip_pairs(lax.axis_size(axis), step))


def chip_return(value, axis, step):
    pairs = chip_pairs(lax.axis_size(axis), step)
    return lax.ppermute(value, axis, [(target, source) for source, target in pairs])


def swap_cores(value, axis):
    count = lax.axis_size(axis)
    return lax.ppermute(value, axis, [(source, source ^ 1) for source in range(count)])


def block_kernel(slots_ref, q_ref, do_ref, code_ref, near_ref, far_ref, dq_ref, dkv_ref,
                 k_sel, v_sel, *, inv_root, heads_here):
    step = pl.program_id(0)
    slots = k_sel.shape[0] // BLOCK
    half, per_tile = near_ref.shape[0], near_ref.shape[2] // BLOCK

    @pl.when(step == 0)
    def _():
        dkv_ref[...] = jnp.zeros_like(dkv_ref)

    for slot in range(slots):
        tile = slots_ref[step, slot] // per_tile
        row = pl.multiple_of(slots_ref[step, slot] % per_tile * BLOCK, BLOCK)
        target = slice(slot * BLOCK, (slot + 1) * BLOCK)

        inside = tile < half
        here = jnp.minimum(tile, half - 1)
        there = jnp.maximum(tile - half, 0)
        k_sel[target, :] = jnp.where(
            inside, near_ref[here, 0, pl.ds(row, BLOCK), :], far_ref[there, 0, pl.ds(row, BLOCK), :]
        )
        v_sel[target, :] = jnp.where(
            inside, near_ref[here, 1, pl.ds(row, BLOCK), :], far_ref[there, 1, pl.ds(row, BLOCK), :]
        )
    q = q_ref[...]
    do = do_ref[...]
    keys = k_sel[...]
    values = v_sel[...]
    rows, cols = q.shape[0], keys.shape[0]
    scores = lax.dot_general(
        q, keys, (((1,), (1,)), ((), ())), preferred_element_type=jnp.float32
    ) * inv_root
    query_pos = lax.broadcasted_iota(jnp.int32, (rows, 1), 0) // heads_here
    allowed = query_pos >= code_ref[...]
    scores = jnp.where(allowed, scores, -1e30)
    row_max = jnp.max(scores, axis=1, keepdims=True)
    shifted = jnp.exp(scores - row_max)
    weights = shifted * (1.0 / jnp.sum(shifted, axis=1, keepdims=True))
    weights_b = weights.astype(jnp.bfloat16)
    output = jnp.dot(weights_b, values, preferred_element_type=jnp.float32)
    row_delta = jnp.sum(do.astype(jnp.float32) * output, axis=1, keepdims=True)
    prob_grad = lax.dot_general(
        do, values, (((1,), (1,)), ((), ())), preferred_element_type=jnp.float32
    )
    score_b = (weights * (prob_grad - row_delta)).astype(jnp.bfloat16)
    query_part = jnp.dot(score_b, keys, preferred_element_type=jnp.float32) * inv_root
    dq_ref[...] = query_part.astype(jnp.bfloat16)
    key_part = lax.dot_general(
        score_b, q, (((0,), (0,)), ((), ())), preferred_element_type=jnp.float32
    ) * inv_root
    value_part = lax.dot_general(
        weights_b, do, (((0,), (0,)), ((), ())), preferred_element_type=jnp.float32
    )
    for slot in range(slots):
        start = pl.multiple_of(slots_ref[step, slot] * BLOCK, BLOCK)
        dkv_ref[0, pl.ds(start, BLOCK), :] += key_part[slot * BLOCK:(slot + 1) * BLOCK]
        dkv_ref[1, pl.ds(start, BLOCK), :] += value_part[slot * BLOCK:(slot + 1) * BLOCK]


def local_grads(queries, out_grad, near, far, slot_index, code, inv_root, interpret=False):
    tokens_here, heads_here, width = queries.shape
    blocks_here, slots = slot_index.shape
    rows = BLOCK * heads_here
    store = (near.shape[0] + far.shape[0]) * near.shape[2]
    cols = slots * BLOCK
    key_pos = jnp.tile(jnp.arange(BLOCK, dtype=jnp.int32), slots)[None, :]
    code_cols = jnp.repeat(code.astype(jnp.int32), BLOCK, axis=1)
    code_cols = jnp.where(code_cols == 2, 0, jnp.where(code_cols == 1, key_pos, BLOCK))
    code_cols = code_cols.reshape(blocks_here, 1, cols)
    kernel = functools.partial(block_kernel, inv_root=inv_root, heads_here=heads_here)
    whole = lambda step, slots_ref: (0, 0)
    per_block = lambda step, slots_ref: (step, 0)
    query_grad, grads = pl.pallas_call(
        kernel,
        grid_spec=pltpu.PrefetchScalarGridSpec(
            num_scalar_prefetch=1,
            grid=(blocks_here,),
            in_specs=[
                pl.BlockSpec((rows, width), per_block),
                pl.BlockSpec((rows, width), per_block),
                pl.BlockSpec((None, 1, cols), lambda step, slots_ref: (step, 0, 0)),
                pl.BlockSpec(near.shape, lambda step, slots_ref: (0, 0, 0, 0)),
                pl.BlockSpec(far.shape, lambda step, slots_ref: (0, 0, 0, 0)),
            ],
            out_specs=[
                pl.BlockSpec((rows, width), per_block),
                pl.BlockSpec((2, store, width), lambda step, slots_ref: (0, 0, 0)),
            ],
            scratch_shapes=[
                pltpu.VMEM((cols, width), jnp.bfloat16),
                pltpu.VMEM((cols, width), jnp.bfloat16),
            ],
        ),
        out_shape=[
            jax.ShapeDtypeStruct((tokens_here * heads_here, width), jnp.bfloat16),
            jax.ShapeDtypeStruct((2, store, width), jnp.float32),
        ],
        compiler_params=pltpu.CompilerParams(dimension_semantics=("arbitrary",)),
        interpret=interpret,
    )(
        slot_index.astype(jnp.int32),
        queries.reshape(tokens_here * heads_here, width),
        out_grad.reshape(tokens_here * heads_here, width),
        code_cols,
        near,
        far,
    )
    return query_grad.reshape(tokens_here, heads_here, width), grads


def per_device(queries, key_rows, value_rows, out_grad, selected, live_slots):
    tokens_here, heads_here, width = queries.shape
    groups = key_rows.shape[0]
    blocks_here = tokens_here // BLOCK
    reach_span = REACH + 1
    inv_root = width ** (-0.5)
    ctx_index = lax.axis_index("ctx")
    group_index = lax.axis_index("grp")
    part_index = lax.axis_index("sub")
    parts_count = lax.axis_size("sub")
    quarter = tokens_here // parts_count
    own_tiles = jnp.stack(
        [
            lax.dynamic_index_in_dim(key_rows, group_index, 0, keepdims=False),
            lax.dynamic_index_in_dim(value_rows, group_index, 0, keepdims=False),
        ]
    )
    rolled = jnp.roll(own_tiles, -part_index * quarter, axis=1)
    own_part = rolled[:, :quarter]
    even = ctx_index % 2 == 0
    took = jnp.stack([chip_fetch(own_part, "ctx", step) for step in range(1, 4)])
    pieces = [took] + [cycled(took, "sub", -step) for step in range(1, parts_count)]
    took = jnp.concatenate(pieces, axis=2)
    mine = jnp.concatenate([rolled[None], took], axis=0)
    partner_tiles = swap_cores(mine, "ctx")
    store_span = 2 * mine.shape[0]
    chosen = lax.dynamic_index_in_dim(selected, group_index, 1, keepdims=False)
    live_mask = lax.dynamic_index_in_dim(live_slots, group_index, 1, keepdims=False)
    block_ids = ctx_index * blocks_here + jnp.arange(blocks_here, dtype=jnp.int32)
    local_block = chosen % blocks_here
    per_part = blocks_here // parts_count
    rolled_block = (local_block // per_part - part_index) % parts_count * per_part + local_block % per_part
    offset = jnp.clip(ctx_index - chosen // blocks_here, 0, REACH)
    placed = jnp.where(
        even, jnp.array([0, 1, 5, 2, 6, 3, 7], jnp.int32)[offset], jnp.array([0, 4, 5, 1, 6, 2, 7], jnp.int32)[offset]
    )
    slot_index = placed * blocks_here + rolled_block
    code = jnp.where(live_mask == 1, jnp.where(chosen < block_ids[:, None], 2, 1), 0)
    query_grad, grads = local_grads(
        queries, out_grad, mine, partner_tiles, slot_index, code, inv_root
    )
    grads = grads.reshape(2, store_span, tokens_here, width)
    half = store_span // 2
    back = swap_cores(grads[:, half:].astype(jnp.bfloat16), "ctx").astype(jnp.float32)
    totals = grads[:, :half] + back
    sent = totals.astype(jnp.bfloat16)

    def reduce_parts(lo, hi):
        part = totals[:, lo:hi, :quarter]
        for step in range(1, parts_count):
            piece = sent[:, lo:hi, step * quarter:(step + 1) * quarter]
            part = part + cycled(piece, "sub", step).astype(jnp.float32)
        return part

    reduced = reduce_parts(0, half)
    running = reduced[:, 0]
    for step in range(1, half):
        term = reduced[:, step].astype(jnp.bfloat16)
        running = running + chip_return(term, "ctx", step).astype(jnp.float32)
    mine = running.astype(jnp.bfloat16)
    by_group = jnp.stack([mine] + [cycled(mine, "grp", -step) for step in range(1, groups)])
    by_part = jnp.stack([by_group] + [cycled(by_group, "sub", -step) for step in range(1, parts_count)])
    part_order = (jnp.arange(parts_count) - part_index) % parts_count
    group_order = (jnp.arange(groups) - group_index) % groups
    flat_order = (part_order[None, :] * groups + group_order[:, None]).reshape(-1)
    ordered = jnp.take(by_part.reshape((parts_count * groups,) + mine.shape), flat_order, axis=0)
    ordered = ordered.reshape((groups, parts_count) + mine.shape)
    summed = jnp.transpose(ordered, (2, 0, 1, 3, 4)).reshape(2, groups, tokens_here, width)
    summed = summed.astype(jnp.float32)
    return (query_grad, summed[0], summed[1])


def solution(mesh):
    ctx_count, head_count = mesh.devices.shape
    groups = 4
    split = Mesh(
        np.asarray(mesh.devices).reshape(ctx_count, groups, head_count // groups),
        ("ctx", "grp", "sub"),
    )
    heads = ("grp", "sub")
    return jax.shard_map(
        per_device,
        mesh=split,
        in_specs=(
            P("ctx", heads, None),
            P(None, "ctx", None),
            P(None, "ctx", None),
            P("ctx", heads, None),
            P("ctx", None, None),
            P("ctx", None, None),
        ),
        out_specs=(P("ctx", heads, None), P(None, "ctx", None), P(None, "ctx", None)),
        check_vma=False,
    )
```

```python
import functools

import jax
import jax.numpy as jnp
import numpy as np
from jax import lax
from jax.experimental import pallas as pl
from jax.experimental.pallas import tpu as pltpu
from jax.sharding import Mesh
from jax.sharding import PartitionSpec as P

HPG = 16
BLOCK = 64
REACH = 6


def cycled(value, axis, steps):
    count = lax.axis_size(axis)
    return lax.ppermute(value, axis, [(source, (source + steps) % count) for source in range(count)])


def chip_pairs(count, step):
    nearer = [(target - (2 * step - 1), target) for target in range(0, count, 2)]
    farther = [(target - (2 * step + 1), target) for target in range(1, count, 2)]
    return [(source, target) for source, target in nearer + farther if source >= 0]


def chip_fetch(value, axis, step):
    return lax.ppermute(value, axis, chip_pairs(lax.axis_size(axis), step))


def chip_return(value, axis, step):
    pairs = chip_pairs(lax.axis_size(axis), step)
    return lax.ppermute(value, axis, [(target, source) for source, target in pairs])


def swap_cores(value, axis):
    count = lax.axis_size(axis)
    return lax.ppermute(value, axis, [(source, source ^ 1) for source in range(count)])


def block_kernel(slots_ref, q_ref, do_ref, code_ref, k_ref, v_ref, dq_ref, dk_ref, dv_ref,
                 k_sel, v_sel, *, inv_root, heads_here):
    step = pl.program_id(0)
    slots = k_sel.shape[0] // BLOCK

    @pl.when(step == 0)
    def _():
        dk_ref[...] = jnp.zeros_like(dk_ref)
        dv_ref[...] = jnp.zeros_like(dv_ref)

    for slot in range(slots):
        start = pl.multiple_of(slots_ref[step, slot] * BLOCK, BLOCK)
        k_sel[slot * BLOCK:(slot + 1) * BLOCK, :] = k_ref[pl.ds(start, BLOCK), :]
        v_sel[slot * BLOCK:(slot + 1) * BLOCK, :] = v_ref[pl.ds(start, BLOCK), :]
    q = q_ref[...]
    do = do_ref[...]
    keys = k_sel[...]
    values = v_sel[...]
    rows, cols = q.shape[0], keys.shape[0]
    scores = lax.dot_general(
        q, keys, (((1,), (1,)), ((), ())), preferred_element_type=jnp.float32
    ) * inv_root
    query_pos = lax.broadcasted_iota(jnp.int32, (rows, 1), 0) // heads_here
    allowed = query_pos >= code_ref[...]
    scores = jnp.where(allowed, scores, -1e30)
    row_max = jnp.max(scores, axis=1, keepdims=True)
    shifted = jnp.exp(scores - row_max)
    weights = shifted * (1.0 / jnp.sum(shifted, axis=1, keepdims=True))
    weights_b = weights.astype(jnp.bfloat16)
    output = jnp.dot(weights_b, values, preferred_element_type=jnp.float32)
    row_delta = jnp.sum(do.astype(jnp.float32) * output, axis=1, keepdims=True)
    prob_grad = lax.dot_general(
        do, values, (((1,), (1,)), ((), ())), preferred_element_type=jnp.float32
    )
    score_b = (weights * (prob_grad - row_delta)).astype(jnp.bfloat16)
    query_part = jnp.dot(score_b, keys, preferred_element_type=jnp.float32) * inv_root
    dq_ref[...] = query_part.astype(jnp.bfloat16)
    key_part = lax.dot_general(
        score_b, q, (((0,), (0,)), ((), ())), preferred_element_type=jnp.float32
    ) * inv_root
    value_part = lax.dot_general(
        weights_b, do, (((0,), (0,)), ((), ())), preferred_element_type=jnp.float32
    )
    for slot in range(slots):
        start = pl.multiple_of(slots_ref[step, slot] * BLOCK, BLOCK)
        dk_ref[pl.ds(start, BLOCK), :] += key_part[slot * BLOCK:(slot + 1) * BLOCK]
        dv_ref[pl.ds(start, BLOCK), :] += value_part[slot * BLOCK:(slot + 1) * BLOCK]


def local_grads(queries, out_grad, key_tiles, value_tiles, slot_index, code, inv_root,
                interpret=False):
    tokens_here, heads_here, width = queries.shape
    blocks_here, slots = slot_index.shape
    rows = BLOCK * heads_here
    store = key_tiles.shape[0] * BLOCK
    cols = slots * BLOCK
    key_pos = jnp.tile(jnp.arange(BLOCK, dtype=jnp.int32), slots)[None, :]
    code_cols = jnp.repeat(code.astype(jnp.int32), BLOCK, axis=1)
    code_cols = jnp.where(code_cols == 2, 0, jnp.where(code_cols == 1, key_pos, BLOCK))
    code_cols = code_cols.reshape(blocks_here, 1, cols)
    kernel = functools.partial(block_kernel, inv_root=inv_root, heads_here=heads_here)
    whole = lambda step, slots_ref: (0, 0)
    per_block = lambda step, slots_ref: (step, 0)
    query_grad, key_grad, value_grad = pl.pallas_call(
        kernel,
        grid_spec=pltpu.PrefetchScalarGridSpec(
            num_scalar_prefetch=1,
            grid=(blocks_here,),
            in_specs=[
                pl.BlockSpec((rows, width), per_block),
                pl.BlockSpec((rows, width), per_block),
                pl.BlockSpec((None, 1, cols), lambda step, slots_ref: (step, 0, 0)),
                pl.BlockSpec((store, width), whole),
                pl.BlockSpec((store, width), whole),
            ],
            out_specs=[
                pl.BlockSpec((rows, width), per_block),
                pl.BlockSpec((store, width), whole),
                pl.BlockSpec((store, width), whole),
            ],
            scratch_shapes=[
                pltpu.VMEM((cols, width), jnp.bfloat16),
                pltpu.VMEM((cols, width), jnp.bfloat16),
            ],
        ),
        out_shape=[
            jax.ShapeDtypeStruct((tokens_here * heads_here, width), jnp.bfloat16),
            jax.ShapeDtypeStruct((store, width), jnp.float32),
            jax.ShapeDtypeStruct((store, width), jnp.float32),
        ],
        compiler_params=pltpu.CompilerParams(dimension_semantics=("arbitrary",)),
        interpret=interpret,
    )(
        slot_index.astype(jnp.int32),
        queries.reshape(tokens_here * heads_here, width),
        out_grad.reshape(tokens_here * heads_here, width),
        code_cols,
        key_tiles.reshape(store, width),
        value_tiles.reshape(store, width),
    )
    return query_grad.reshape(tokens_here, heads_here, width), key_grad, value_grad


def per_device(queries, key_rows, value_rows, out_grad, selected, live_slots):
    tokens_here, heads_here, width = queries.shape
    groups = key_rows.shape[0]
    blocks_here = tokens_here // BLOCK
    reach_span = REACH + 1
    inv_root = width ** (-0.5)
    ctx_index = lax.axis_index("ctx")
    group_index = lax.axis_index("grp")
    part_index = lax.axis_index("sub")
    parts_count = lax.axis_size("sub")
    quarter = tokens_here // parts_count
    own_tiles = jnp.stack(
        [
            lax.dynamic_index_in_dim(key_rows, group_index, 0, keepdims=False),
            lax.dynamic_index_in_dim(value_rows, group_index, 0, keepdims=False),
        ]
    )
    rolled = jnp.roll(own_tiles, -part_index * quarter, axis=1)
    own_part = rolled[:, :quarter]
    even = ctx_index % 2 == 0
    took = jnp.stack([chip_fetch(own_part, "ctx", step) for step in range(1, 4)])
    pieces = [took] + [cycled(took, "sub", -step) for step in range(1, parts_count)]
    took = jnp.concatenate(pieces, axis=2)
    mine = jnp.concatenate([rolled[None], took], axis=0)
    tile_store = jnp.concatenate([mine, swap_cores(mine, "ctx")], axis=0)
    store_span = tile_store.shape[0]
    key_tiles = tile_store[:, 0].reshape(store_span * blocks_here, BLOCK, width)
    value_tiles = tile_store[:, 1].reshape(store_span * blocks_here, BLOCK, width)
    chosen = lax.dynamic_index_in_dim(selected, group_index, 1, keepdims=False)
    live_mask = lax.dynamic_index_in_dim(live_slots, group_index, 1, keepdims=False)
    block_ids = ctx_index * blocks_here + jnp.arange(blocks_here, dtype=jnp.int32)
    local_block = chosen % blocks_here
    per_part = blocks_here // parts_count
    rolled_block = (local_block // per_part - part_index) % parts_count * per_part + local_block % per_part
    offset = jnp.clip(ctx_index - chosen // blocks_here, 0, REACH)
    placed = jnp.where(
        even, jnp.array([0, 1, 5, 2, 6, 3, 7], jnp.int32)[offset], jnp.array([0, 4, 5, 1, 6, 2, 7], jnp.int32)[offset]
    )
    slot_index = placed * blocks_here + rolled_block
    code = jnp.where(live_mask == 1, jnp.where(chosen < block_ids[:, None], 2, 1), 0)
    query_grad, key_grad, value_grad = local_grads(
        queries, out_grad, key_tiles, value_tiles, slot_index, code, inv_root
    )
    grads = jnp.stack([key_grad, value_grad]).reshape(2, store_span, tokens_here, width)
    half = store_span // 2
    back = swap_cores(grads[:, half:], "ctx")
    totals = grads[:, :half] + back
    sent = totals.astype(jnp.bfloat16)

    def reduce_parts(lo, hi):
        part = totals[:, lo:hi, :quarter]
        for step in range(1, parts_count):
            piece = sent[:, lo:hi, step * quarter:(step + 1) * quarter]
            part = part + cycled(piece, "sub", step).astype(jnp.float32)
        return part

    reduced = reduce_parts(0, half)
    running = reduced[:, 0]
    for step in range(1, half):
        term = reduced[:, step].astype(jnp.bfloat16)
        running = running + chip_return(term, "ctx", step).astype(jnp.float32)
    mine = running.astype(jnp.bfloat16)
    by_group = jnp.stack([mine] + [cycled(mine, "grp", -step) for step in range(1, groups)])
    by_part = jnp.stack([by_group] + [cycled(by_group, "sub", -step) for step in range(1, parts_count)])
    part_order = (jnp.arange(parts_count) - part_index) % parts_count
    group_order = (jnp.arange(groups) - group_index) % groups
    flat_order = (part_order[None, :] * groups + group_order[:, None]).reshape(-1)
    ordered = jnp.take(by_part.reshape((parts_count * groups,) + mine.shape), flat_order, axis=0)
    ordered = ordered.reshape((groups, parts_count) + mine.shape)
    summed = jnp.transpose(ordered, (2, 0, 1, 3, 4)).reshape(2, groups, tokens_here, width)
    summed = summed.astype(jnp.float32)
    return (query_grad, summed[0], summed[1])


def solution(mesh):
    ctx_count, head_count = mesh.devices.shape
    groups = 4
    split = Mesh(
        np.asarray(mesh.devices).reshape(ctx_count, groups, head_count // groups),
        ("ctx", "grp", "sub"),
    )
    heads = ("grp", "sub")
    return jax.shard_map(
        per_device,
        mesh=split,
        in_specs=(
            P("ctx", heads, None),
            P(None, "ctx", None),
            P(None, "ctx", None),
            P("ctx", heads, None),
            P("ctx", None, None),
            P("ctx", None, None),
        ),
        out_specs=(P("ctx", heads, None), P(None, "ctx", None), P(None, "ctx", None)),
        check_vma=False,
    )
```

```python
import functools

import jax
import jax.numpy as jnp
import numpy as np
from jax import lax
from jax.experimental import pallas as pl
from jax.experimental.pallas import tpu as pltpu
from jax.sharding import Mesh
from jax.sharding import PartitionSpec as P

HPG = 16
BLOCK = 64
REACH = 6


def cycled(value, axis, steps):
    count = lax.axis_size(axis)
    return lax.ppermute(value, axis, [(source, (source + steps) % count) for source in range(count)])


def chip_pairs(count, step):
    nearer = [(target - (2 * step - 1), target) for target in range(0, count, 2)]
    farther = [(target - (2 * step + 1), target) for target in range(1, count, 2)]
    return [(source, target) for source, target in nearer + farther if source >= 0]


def chip_fetch(value, axis, step):
    return lax.ppermute(value, axis, chip_pairs(lax.axis_size(axis), step))


def chip_return(value, axis, step):
    pairs = chip_pairs(lax.axis_size(axis), step)
    return lax.ppermute(value, axis, [(target, source) for source, target in pairs])


def swap_cores(value, axis):
    count = lax.axis_size(axis)
    return lax.ppermute(value, axis, [(source, source ^ 1) for source in range(count)])


def block_kernel(slots_ref, q_ref, do_ref, code_ref, k_ref, v_ref, dq_ref, dk_ref, dv_ref,
                 k_sel, v_sel, *, inv_root, heads_here):
    step = pl.program_id(0)
    slots = k_sel.shape[0] // BLOCK

    @pl.when(step == 0)
    def _():
        dk_ref[...] = jnp.zeros_like(dk_ref)
        dv_ref[...] = jnp.zeros_like(dv_ref)

    for slot in range(slots):
        start = pl.multiple_of(slots_ref[step, slot] * BLOCK, BLOCK)
        k_sel[slot * BLOCK:(slot + 1) * BLOCK, :] = k_ref[pl.ds(start, BLOCK), :]
        v_sel[slot * BLOCK:(slot + 1) * BLOCK, :] = v_ref[pl.ds(start, BLOCK), :]
    q = q_ref[...]
    do = do_ref[...]
    keys = k_sel[...]
    values = v_sel[...]
    rows, cols = q.shape[0], keys.shape[0]
    scores = lax.dot_general(
        q, keys, (((1,), (1,)), ((), ())), preferred_element_type=jnp.float32
    ) * inv_root
    query_pos = lax.broadcasted_iota(jnp.int32, (rows, 1), 0) // heads_here
    allowed = query_pos >= code_ref[...]
    scores = jnp.where(allowed, scores, -1e30)
    row_max = jnp.max(scores, axis=1, keepdims=True)
    shifted = jnp.exp(scores - row_max)
    weights = shifted * (1.0 / jnp.sum(shifted, axis=1, keepdims=True))
    weights_b = weights.astype(jnp.bfloat16)
    output = jnp.dot(weights_b, values, preferred_element_type=jnp.float32)
    row_delta = jnp.sum(do.astype(jnp.float32) * output, axis=1, keepdims=True)
    prob_grad = lax.dot_general(
        do, values, (((1,), (1,)), ((), ())), preferred_element_type=jnp.float32
    )
    score_b = (weights * (prob_grad - row_delta)).astype(jnp.bfloat16)
    query_part = jnp.dot(score_b, keys, preferred_element_type=jnp.float32) * inv_root
    dq_ref[...] = query_part.astype(jnp.bfloat16)
    key_part = lax.dot_general(
        score_b, q, (((0,), (0,)), ((), ())), preferred_element_type=jnp.float32
    ) * inv_root
    value_part = lax.dot_general(
        weights_b, do, (((0,), (0,)), ((), ())), preferred_element_type=jnp.float32
    )
    for slot in range(slots):
        start = pl.multiple_of(slots_ref[step, slot] * BLOCK, BLOCK)
        dk_ref[pl.ds(start, BLOCK), :] += key_part[slot * BLOCK:(slot + 1) * BLOCK]
        dv_ref[pl.ds(start, BLOCK), :] += value_part[slot * BLOCK:(slot + 1) * BLOCK]


def local_grads(queries, out_grad, key_tiles, value_tiles, slot_index, code, inv_root,
                interpret=False):
    tokens_here, heads_here, width = queries.shape
    blocks_here, slots = slot_index.shape
    rows = BLOCK * heads_here
    store = key_tiles.shape[0] * BLOCK
    cols = slots * BLOCK
    key_pos = jnp.tile(jnp.arange(BLOCK, dtype=jnp.int32), slots)[None, :]
    code_cols = jnp.repeat(code.astype(jnp.int32), BLOCK, axis=1)
    code_cols = jnp.where(code_cols == 2, 0, jnp.where(code_cols == 1, key_pos, BLOCK))
    code_cols = code_cols.reshape(blocks_here, 1, cols)
    kernel = functools.partial(block_kernel, inv_root=inv_root, heads_here=heads_here)
    whole = lambda step, slots_ref: (0, 0)
    per_block = lambda step, slots_ref: (step, 0)
    query_grad, key_grad, value_grad = pl.pallas_call(
        kernel,
        grid_spec=pltpu.PrefetchScalarGridSpec(
            num_scalar_prefetch=1,
            grid=(blocks_here,),
            in_specs=[
                pl.BlockSpec((rows, width), per_block),
                pl.BlockSpec((rows, width), per_block),
                pl.BlockSpec((None, 1, cols), lambda step, slots_ref: (step, 0, 0)),
                pl.BlockSpec((store, width), whole),
                pl.BlockSpec((store, width), whole),
            ],
            out_specs=[
                pl.BlockSpec((rows, width), per_block),
                pl.BlockSpec((store, width), whole),
                pl.BlockSpec((store, width), whole),
            ],
            scratch_shapes=[
                pltpu.VMEM((cols, width), jnp.bfloat16),
                pltpu.VMEM((cols, width), jnp.bfloat16),
            ],
        ),
        out_shape=[
            jax.ShapeDtypeStruct((tokens_here * heads_here, width), jnp.bfloat16),
            jax.ShapeDtypeStruct((store, width), jnp.float32),
            jax.ShapeDtypeStruct((store, width), jnp.float32),
        ],
        compiler_params=pltpu.CompilerParams(dimension_semantics=("arbitrary",)),
        interpret=interpret,
    )(
        slot_index.astype(jnp.int32),
        queries.reshape(tokens_here * heads_here, width),
        out_grad.reshape(tokens_here * heads_here, width),
        code_cols,
        key_tiles.reshape(store, width),
        value_tiles.reshape(store, width),
    )
    return query_grad.reshape(tokens_here, heads_here, width), key_grad, value_grad


def per_device(queries, key_rows, value_rows, out_grad, selected, live_slots):
    tokens_here, heads_here, width = queries.shape
    groups = key_rows.shape[0]
    blocks_here = tokens_here // BLOCK
    reach_span = REACH + 1
    inv_root = width ** (-0.5)
    ctx_index = lax.axis_index("ctx")
    group_index = lax.axis_index("grp")
    part_index = lax.axis_index("sub")
    parts_count = lax.axis_size("sub")
    quarter = tokens_here // parts_count
    own_tiles = jnp.stack(
        [
            lax.dynamic_index_in_dim(key_rows, group_index, 0, keepdims=False),
            lax.dynamic_index_in_dim(value_rows, group_index, 0, keepdims=False),
        ]
    )
    rolled = jnp.roll(own_tiles, -part_index * quarter, axis=1)
    own_part = rolled[:, :quarter]
    even = ctx_index % 2 == 0
    took = [chip_fetch(own_part, "ctx", step) for step in range(1, 3)]
    took = jnp.stack(took + [chip_fetch(took[1], "ctx", 1)])
    pieces = [took] + [cycled(took, "sub", -step) for step in range(1, parts_count)]
    took = jnp.concatenate(pieces, axis=2)
    mine = jnp.concatenate([rolled[None], took], axis=0)
    tile_store = jnp.concatenate([mine, swap_cores(mine, "ctx")], axis=0)
    store_span = tile_store.shape[0]
    key_tiles = tile_store[:, 0].reshape(store_span * blocks_here, BLOCK, width)
    value_tiles = tile_store[:, 1].reshape(store_span * blocks_here, BLOCK, width)
    chosen = lax.dynamic_index_in_dim(selected, group_index, 1, keepdims=False)
    live_mask = lax.dynamic_index_in_dim(live_slots, group_index, 1, keepdims=False)
    block_ids = ctx_index * blocks_here + jnp.arange(blocks_here, dtype=jnp.int32)
    local_block = chosen % blocks_here
    per_part = blocks_here // parts_count
    rolled_block = (local_block // per_part - part_index) % parts_count * per_part + local_block % per_part
    offset = jnp.clip(ctx_index - chosen // blocks_here, 0, REACH)
    placed = jnp.where(
        even, jnp.array([0, 1, 5, 2, 6, 7, 3], jnp.int32)[offset], jnp.array([0, 4, 5, 1, 6, 2, 3], jnp.int32)[offset]
    )
    slot_index = placed * blocks_here + rolled_block
    code = jnp.where(live_mask == 1, jnp.where(chosen < block_ids[:, None], 2, 1), 0)
    query_grad, key_grad, value_grad = local_grads(
        queries, out_grad, key_tiles, value_tiles, slot_index, code, inv_root
    )
    grads = jnp.stack([key_grad, value_grad]).reshape(2, store_span, tokens_here, width)
    half = store_span // 2
    back = swap_cores(grads[:, half:].astype(jnp.bfloat16), "ctx").astype(jnp.float32)
    totals = grads[:, :half] + back
    sent = totals.astype(jnp.bfloat16)

    def reduce_parts(lo, hi):
        part = totals[:, lo:hi, :quarter]
        for step in range(1, parts_count):
            piece = sent[:, lo:hi, step * quarter:(step + 1) * quarter]
            part = part + cycled(piece, "sub", step).astype(jnp.float32)
        return part

    reduced = reduce_parts(0, half)
    running = reduced[:, 0]
    for step in range(1, half - 1):
        term = reduced[:, step].astype(jnp.bfloat16)
        running = running + chip_return(term, "ctx", step).astype(jnp.float32)
    count = lax.axis_size("ctx")
    farthest = lax.ppermute(
        reduced[:, half - 1].astype(jnp.bfloat16), "ctx",
        [(source, source - REACH) for source in range(REACH, count)],
    )
    running = running + farthest.astype(jnp.float32)
    mine = running.astype(jnp.bfloat16)
    by_group = jnp.stack([mine] + [cycled(mine, "grp", -step) for step in range(1, groups)])
    by_part = jnp.stack([by_group] + [cycled(by_group, "sub", -step) for step in range(1, parts_count)])
    part_order = (jnp.arange(parts_count) - part_index) % parts_count
    group_order = (jnp.arange(groups) - group_index) % groups
    flat_order = (part_order[None, :] * groups + group_order[:, None]).reshape(-1)
    ordered = jnp.take(by_part.reshape((parts_count * groups,) + mine.shape), flat_order, axis=0)
    ordered = ordered.reshape((groups, parts_count) + mine.shape)
    summed = jnp.transpose(ordered, (2, 0, 1, 3, 4)).reshape(2, groups, tokens_here, width)
    summed = summed.astype(jnp.float32)
    return (query_grad, summed[0], summed[1])


def solution(mesh):
    ctx_count, head_count = mesh.devices.shape
    groups = 4
    split = Mesh(
        np.asarray(mesh.devices).reshape(ctx_count, groups, head_count // groups),
        ("ctx", "grp", "sub"),
    )
    heads = ("grp", "sub")
    return jax.shard_map(
        per_device,
        mesh=split,
        in_specs=(
            P("ctx", heads, None),
            P(None, "ctx", None),
            P(None, "ctx", None),
            P("ctx", heads, None),
            P("ctx", None, None),
            P("ctx", None, None),
        ),
        out_specs=(P("ctx", heads, None), P(None, "ctx", None), P(None, "ctx", None)),
        check_vma=False,
    )
```

```python
import functools

import jax
import jax.numpy as jnp
import numpy as np
from jax import lax
from jax.experimental import pallas as pl
from jax.experimental.pallas import tpu as pltpu
from jax.sharding import Mesh
from jax.sharding import PartitionSpec as P

HPG = 16
BLOCK = 64
REACH = 6


def cycled(value, axis, steps):
    count = lax.axis_size(axis)
    return lax.ppermute(value, axis, [(source, (source + steps) % count) for source in range(count)])


def chip_pairs(count, step):
    nearer = [(target - (2 * step - 1), target) for target in range(0, count, 2)]
    farther = [(target - (2 * step + 1), target) for target in range(1, count, 2)]
    return [(source, target) for source, target in nearer + farther if source >= 0]


def chip_fetch(value, axis, step):
    return lax.ppermute(value, axis, chip_pairs(lax.axis_size(axis), step))


def chip_return(value, axis, step):
    pairs = chip_pairs(lax.axis_size(axis), step)
    return lax.ppermute(value, axis, [(target, source) for source, target in pairs])


def swap_cores(value, axis):
    count = lax.axis_size(axis)
    return lax.ppermute(value, axis, [(source, source ^ 1) for source in range(count)])


def block_kernel(slots_ref, q_ref, do_ref, code_ref, k_ref, v_ref, dq_ref, dk_ref, dv_ref,
                 k_sel, v_sel, *, inv_root, heads_here):
    step = pl.program_id(0)
    slots = k_sel.shape[0] // BLOCK

    @pl.when(step == 0)
    def _():
        dk_ref[...] = jnp.zeros_like(dk_ref)
        dv_ref[...] = jnp.zeros_like(dv_ref)

    for slot in range(slots):
        start = pl.multiple_of(slots_ref[step, slot] * BLOCK, BLOCK)
        k_sel[slot * BLOCK:(slot + 1) * BLOCK, :] = k_ref[pl.ds(start, BLOCK), :]
        v_sel[slot * BLOCK:(slot + 1) * BLOCK, :] = v_ref[pl.ds(start, BLOCK), :]
    q = q_ref[...]
    do = do_ref[...]
    keys = k_sel[...]
    values = v_sel[...]
    rows, cols = q.shape[0], keys.shape[0]
    scores = lax.dot_general(
        q, keys, (((1,), (1,)), ((), ())), preferred_element_type=jnp.float32
    ) * inv_root
    query_pos = lax.broadcasted_iota(jnp.int32, (rows, 1), 0) // heads_here
    allowed = query_pos >= code_ref[...]
    scores = jnp.where(allowed, scores, -1e30)
    row_max = jnp.max(scores, axis=1, keepdims=True)
    shifted = jnp.exp(scores - row_max)
    weights = shifted * (1.0 / jnp.sum(shifted, axis=1, keepdims=True))
    weights_b = weights.astype(jnp.bfloat16)
    output = jnp.dot(weights_b, values, preferred_element_type=jnp.float32)
    row_delta = jnp.sum(do.astype(jnp.float32) * output, axis=1, keepdims=True)
    prob_grad = lax.dot_general(
        do, values, (((1,), (1,)), ((), ())), preferred_element_type=jnp.float32
    )
    score_b = (weights * (prob_grad - row_delta)).astype(jnp.bfloat16)
    query_part = jnp.dot(score_b, keys, preferred_element_type=jnp.float32) * inv_root
    dq_ref[...] = query_part.astype(jnp.bfloat16)
    key_part = lax.dot_general(
        score_b, q, (((0,), (0,)), ((), ())), preferred_element_type=jnp.float32
    ) * inv_root
    value_part = lax.dot_general(
        weights_b, do, (((0,), (0,)), ((), ())), preferred_element_type=jnp.float32
    )
    for slot in range(slots):
        start = pl.multiple_of(slots_ref[step, slot] * BLOCK, BLOCK)
        dk_ref[pl.ds(start, BLOCK), :] += key_part[slot * BLOCK:(slot + 1) * BLOCK]
        dv_ref[pl.ds(start, BLOCK), :] += value_part[slot * BLOCK:(slot + 1) * BLOCK]


def local_grads(queries, out_grad, key_tiles, value_tiles, slot_index, code, inv_root,
                interpret=False):
    tokens_here, heads_here, width = queries.shape
    blocks_here, slots = slot_index.shape
    rows = BLOCK * heads_here
    store = key_tiles.shape[0] * BLOCK
    cols = slots * BLOCK
    key_pos = jnp.tile(jnp.arange(BLOCK, dtype=jnp.int32), slots)[None, :]
    code_cols = jnp.repeat(code.astype(jnp.int32), BLOCK, axis=1)
    code_cols = jnp.where(code_cols == 2, 0, jnp.where(code_cols == 1, key_pos, BLOCK))
    code_cols = code_cols.reshape(blocks_here, 1, cols)
    kernel = functools.partial(block_kernel, inv_root=inv_root, heads_here=heads_here)
    whole = lambda step, slots_ref: (0, 0)
    per_block = lambda step, slots_ref: (step, 0)
    query_grad, key_grad, value_grad = pl.pallas_call(
        kernel,
        grid_spec=pltpu.PrefetchScalarGridSpec(
            num_scalar_prefetch=1,
            grid=(blocks_here,),
            in_specs=[
                pl.BlockSpec((rows, width), per_block),
                pl.BlockSpec((rows, width), per_block),
                pl.BlockSpec((None, 1, cols), lambda step, slots_ref: (step, 0, 0)),
                pl.BlockSpec((store, width), whole),
                pl.BlockSpec((store, width), whole),
            ],
            out_specs=[
                pl.BlockSpec((rows, width), per_block),
                pl.BlockSpec((store, width), whole),
                pl.BlockSpec((store, width), whole),
            ],
            scratch_shapes=[
                pltpu.VMEM((cols, width), jnp.bfloat16),
                pltpu.VMEM((cols, width), jnp.bfloat16),
            ],
        ),
        out_shape=[
            jax.ShapeDtypeStruct((tokens_here * heads_here, width), jnp.bfloat16),
            jax.ShapeDtypeStruct((store, width), jnp.float32),
            jax.ShapeDtypeStruct((store, width), jnp.float32),
        ],
        compiler_params=pltpu.CompilerParams(dimension_semantics=("arbitrary",)),
        interpret=interpret,
    )(
        slot_index.astype(jnp.int32),
        queries.reshape(tokens_here * heads_here, width),
        out_grad.reshape(tokens_here * heads_here, width),
        code_cols,
        key_tiles.reshape(store, width),
        value_tiles.reshape(store, width),
    )
    return query_grad.reshape(tokens_here, heads_here, width), key_grad, value_grad


def per_device(queries, key_rows, value_rows, out_grad, selected, live_slots):
    tokens_here, heads_here, width = queries.shape
    groups = key_rows.shape[0]
    blocks_here = tokens_here // BLOCK
    reach_span = REACH + 1
    inv_root = width ** (-0.5)
    ctx_index = lax.axis_index("ctx")
    group_index = lax.axis_index("grp")
    part_index = lax.axis_index("sub")
    parts_count = lax.axis_size("sub")
    quarter = tokens_here // parts_count
    own_tiles = jnp.stack(
        [
            lax.dynamic_index_in_dim(key_rows, group_index, 0, keepdims=False),
            lax.dynamic_index_in_dim(value_rows, group_index, 0, keepdims=False),
        ]
    )
    rolled = jnp.roll(own_tiles, -part_index * quarter, axis=1)
    own_part = jnp.stack(
        [
            lax.dynamic_slice(rows, (group_index, part_index * quarter, 0), (1, quarter, width))[0]
            for rows in (key_rows, value_rows)
        ]
    )
    even = ctx_index % 2 == 0
    took = jnp.stack([chip_fetch(own_part, "ctx", step) for step in range(1, 4)])
    pieces = [took] + [cycled(took, "sub", -step) for step in range(1, parts_count)]
    took = jnp.concatenate(pieces, axis=2)
    mine = jnp.concatenate([rolled[None], took], axis=0)
    tile_store = jnp.concatenate([mine, swap_cores(mine, "ctx")], axis=0)
    store_span = tile_store.shape[0]
    key_tiles = tile_store[:, 0].reshape(store_span * blocks_here, BLOCK, width)
    value_tiles = tile_store[:, 1].reshape(store_span * blocks_here, BLOCK, width)
    chosen = lax.dynamic_index_in_dim(selected, group_index, 1, keepdims=False)
    live_mask = lax.dynamic_index_in_dim(live_slots, group_index, 1, keepdims=False)
    block_ids = ctx_index * blocks_here + jnp.arange(blocks_here, dtype=jnp.int32)
    local_block = chosen % blocks_here
    per_part = blocks_here // parts_count
    rolled_block = (local_block // per_part - part_index) % parts_count * per_part + local_block % per_part
    offset = jnp.clip(ctx_index - chosen // blocks_here, 0, REACH)
    placed = jnp.where(
        even, jnp.array([0, 1, 5, 2, 6, 3, 7], jnp.int32)[offset], jnp.array([0, 4, 5, 1, 6, 2, 7], jnp.int32)[offset]
    )
    slot_index = placed * blocks_here + rolled_block
    code = jnp.where(live_mask == 1, jnp.where(chosen < block_ids[:, None], 2, 1), 0)
    query_grad, key_grad, value_grad = local_grads(
        queries, out_grad, key_tiles, value_tiles, slot_index, code, inv_root
    )
    grads = jnp.stack([key_grad, value_grad]).reshape(2, store_span, tokens_here, width)
    half = store_span // 2
    back = swap_cores(grads[:, half:].astype(jnp.bfloat16), "ctx").astype(jnp.float32)
    totals = grads[:, :half] + back
    sent = totals.astype(jnp.bfloat16)

    def reduce_parts(lo, hi):
        part = totals[:, lo:hi, :quarter]
        for step in range(1, parts_count):
            piece = sent[:, lo:hi, step * quarter:(step + 1) * quarter]
            part = part + cycled(piece, "sub", step).astype(jnp.float32)
        return part

    reduced = reduce_parts(0, half)
    running = reduced[:, 0]
    for step in range(1, half):
        term = reduced[:, step].astype(jnp.bfloat16)
        running = running + chip_return(term, "ctx", step).astype(jnp.float32)
    mine = running.astype(jnp.bfloat16)
    by_group = jnp.stack([mine] + [cycled(mine, "grp", -step) for step in range(1, groups)])
    by_part = jnp.stack([by_group] + [cycled(by_group, "sub", -step) for step in range(1, parts_count)])
    part_order = (jnp.arange(parts_count) - part_index) % parts_count
    group_order = (jnp.arange(groups) - group_index) % groups
    flat_order = (part_order[None, :] * groups + group_order[:, None]).reshape(-1)
    ordered = jnp.take(by_part.reshape((parts_count * groups,) + mine.shape), flat_order, axis=0)
    ordered = ordered.reshape((groups, parts_count) + mine.shape)
    summed = jnp.transpose(ordered, (2, 0, 1, 3, 4)).reshape(2, groups, tokens_here, width)
    summed = summed.astype(jnp.float32)
    return (query_grad, summed[0], summed[1])


def solution(mesh):
    ctx_count, head_count = mesh.devices.shape
    groups = 4
    split = Mesh(
        np.asarray(mesh.devices).reshape(ctx_count, groups, head_count // groups),
        ("ctx", "grp", "sub"),
    )
    heads = ("grp", "sub")
    return jax.shard_map(
        per_device,
        mesh=split,
        in_specs=(
            P("ctx", heads, None),
            P(None, "ctx", None),
            P(None, "ctx", None),
            P("ctx", heads, None),
            P("ctx", None, None),
            P("ctx", None, None),
        ),
        out_specs=(P("ctx", heads, None), P(None, "ctx", None), P(None, "ctx", None)),
        check_vma=False,
    )
```

```python
import functools

import jax
import jax.numpy as jnp
import numpy as np
from jax import lax
from jax.experimental import pallas as pl
from jax.experimental.pallas import tpu as pltpu
from jax.sharding import Mesh
from jax.sharding import PartitionSpec as P

HPG = 16
BLOCK = 64
REACH = 6


def cycled(value, axis, steps):
    count = lax.axis_size(axis)
    return lax.ppermute(value, axis, [(source, (source + steps) % count) for source in range(count)])


def chip_pairs(count, step):
    nearer = [(target - (2 * step - 1), target) for target in range(0, count, 2)]
    farther = [(target - (2 * step + 1), target) for target in range(1, count, 2)]
    return [(source, target) for source, target in nearer + farther if source >= 0]


def chip_fetch(value, axis, step):
    return lax.ppermute(value, axis, chip_pairs(lax.axis_size(axis), step))


def chip_return(value, axis, step):
    pairs = chip_pairs(lax.axis_size(axis), step)
    return lax.ppermute(value, axis, [(target, source) for source, target in pairs])


def swap_cores(value, axis):
    count = lax.axis_size(axis)
    return lax.ppermute(value, axis, [(source, source ^ 1) for source in range(count)])


def block_kernel(slots_ref, q_ref, do_ref, code_ref, k_ref, v_ref, dq_ref, dk_ref, dv_ref,
                 k_sel, v_sel, *, inv_root, heads_here):
    step = pl.program_id(0)
    slots = k_sel.shape[0] // BLOCK

    @pl.when(step == 0)
    def _():
        dk_ref[...] = jnp.zeros_like(dk_ref)
        dv_ref[...] = jnp.zeros_like(dv_ref)

    pair = code_ref.shape[0]
    rows_each = q_ref.shape[0] // pair
    for part in range(pair):
        for slot in range(slots):
            start = pl.multiple_of(slots_ref[pair * step + part, slot] * BLOCK, BLOCK)
            k_sel[slot * BLOCK:(slot + 1) * BLOCK, :] = k_ref[pl.ds(start, BLOCK), :]
            v_sel[slot * BLOCK:(slot + 1) * BLOCK, :] = v_ref[pl.ds(start, BLOCK), :]
        q = q_ref[part * rows_each:(part + 1) * rows_each, :]
        do = do_ref[part * rows_each:(part + 1) * rows_each, :]
        keys = k_sel[...]
        values = v_sel[...]
        rows, cols = q.shape[0], keys.shape[0]
        scores = lax.dot_general(
            q, keys, (((1,), (1,)), ((), ())), preferred_element_type=jnp.float32
        ) * inv_root
        query_pos = lax.broadcasted_iota(jnp.int32, (rows, 1), 0) // heads_here
        allowed = query_pos >= code_ref[part]
        scores = jnp.where(allowed, scores, -1e30)
        row_max = jnp.max(scores, axis=1, keepdims=True)
        shifted = jnp.exp(scores - row_max)
        weights = shifted * (1.0 / jnp.sum(shifted, axis=1, keepdims=True))
        weights_b = weights.astype(jnp.bfloat16)
        output = jnp.dot(weights_b, values, preferred_element_type=jnp.float32)
        row_delta = jnp.sum(do.astype(jnp.float32) * output, axis=1, keepdims=True)
        prob_grad = lax.dot_general(
            do, values, (((1,), (1,)), ((), ())), preferred_element_type=jnp.float32
        )
        score_b = (weights * (prob_grad - row_delta)).astype(jnp.bfloat16)
        query_part = jnp.dot(score_b, keys, preferred_element_type=jnp.float32) * inv_root
        dq_ref[part * rows_each:(part + 1) * rows_each, :] = query_part.astype(jnp.bfloat16)
        key_part = lax.dot_general(
            score_b, q, (((0,), (0,)), ((), ())), preferred_element_type=jnp.float32
        ) * inv_root
        value_part = lax.dot_general(
            weights_b, do, (((0,), (0,)), ((), ())), preferred_element_type=jnp.float32
        )
        for slot in range(slots):
            start = pl.multiple_of(slots_ref[pair * step + part, slot] * BLOCK, BLOCK)
            dk_ref[pl.ds(start, BLOCK), :] += key_part[slot * BLOCK:(slot + 1) * BLOCK]
            dv_ref[pl.ds(start, BLOCK), :] += value_part[slot * BLOCK:(slot + 1) * BLOCK]


def local_grads(queries, out_grad, key_tiles, value_tiles, slot_index, code, inv_root,
                interpret=False):
    tokens_here, heads_here, width = queries.shape
    blocks_here, slots = slot_index.shape
    rows = 2 * BLOCK * heads_here
    store = key_tiles.shape[0] * BLOCK
    cols = slots * BLOCK
    key_pos = jnp.tile(jnp.arange(BLOCK, dtype=jnp.int32), slots)[None, :]
    code_cols = jnp.repeat(code.astype(jnp.int32), BLOCK, axis=1)
    code_cols = jnp.where(code_cols == 2, 0, jnp.where(code_cols == 1, key_pos, BLOCK))
    code_cols = code_cols.reshape(blocks_here, 1, cols)
    kernel = functools.partial(block_kernel, inv_root=inv_root, heads_here=heads_here)
    whole = lambda step, slots_ref: (0, 0)
    per_block = lambda step, slots_ref: (step, 0)
    query_grad, key_grad, value_grad = pl.pallas_call(
        kernel,
        grid_spec=pltpu.PrefetchScalarGridSpec(
            num_scalar_prefetch=1,
            grid=(blocks_here // 2,),
            in_specs=[
                pl.BlockSpec((rows, width), per_block),
                pl.BlockSpec((rows, width), per_block),
                pl.BlockSpec((2, 1, cols), lambda step, slots_ref: (step, 0, 0)),
                pl.BlockSpec((store, width), whole),
                pl.BlockSpec((store, width), whole),
            ],
            out_specs=[
                pl.BlockSpec((rows, width), per_block),
                pl.BlockSpec((store, width), whole),
                pl.BlockSpec((store, width), whole),
            ],
            scratch_shapes=[
                pltpu.VMEM((cols, width), jnp.bfloat16),
                pltpu.VMEM((cols, width), jnp.bfloat16),
            ],
        ),
        out_shape=[
            jax.ShapeDtypeStruct((tokens_here * heads_here, width), jnp.bfloat16),
            jax.ShapeDtypeStruct((store, width), jnp.float32),
            jax.ShapeDtypeStruct((store, width), jnp.float32),
        ],
        compiler_params=pltpu.CompilerParams(dimension_semantics=("arbitrary",)),
        interpret=interpret,
    )(
        slot_index.astype(jnp.int32),
        queries.reshape(tokens_here * heads_here, width),
        out_grad.reshape(tokens_here * heads_here, width),
        code_cols,
        key_tiles.reshape(store, width),
        value_tiles.reshape(store, width),
    )
    return query_grad.reshape(tokens_here, heads_here, width), key_grad, value_grad


def per_device(queries, key_rows, value_rows, out_grad, selected, live_slots):
    tokens_here, heads_here, width = queries.shape
    groups = key_rows.shape[0]
    blocks_here = tokens_here // BLOCK
    reach_span = REACH + 1
    inv_root = width ** (-0.5)
    ctx_index = lax.axis_index("ctx")
    group_index = lax.axis_index("grp")
    part_index = lax.axis_index("sub")
    parts_count = lax.axis_size("sub")
    quarter = tokens_here // parts_count
    own_tiles = jnp.stack(
        [
            lax.dynamic_index_in_dim(key_rows, group_index, 0, keepdims=False),
            lax.dynamic_index_in_dim(value_rows, group_index, 0, keepdims=False),
        ]
    )
    rolled = jnp.roll(own_tiles, -part_index * quarter, axis=1)
    own_part = jnp.stack(
        [
            lax.dynamic_slice(rows, (group_index, part_index * quarter, 0), (1, quarter, width))[0]
            for rows in (key_rows, value_rows)
        ]
    )
    even = ctx_index % 2 == 0
    took = jnp.stack([chip_fetch(own_part, "ctx", step) for step in range(1, 4)])
    pieces = [took] + [cycled(took, "sub", -step) for step in range(1, parts_count)]
    took = jnp.concatenate(pieces, axis=2)
    mine = jnp.concatenate([rolled[None], took], axis=0)
    tile_store = jnp.concatenate([mine, swap_cores(mine, "ctx")], axis=0)
    store_span = tile_store.shape[0]
    key_tiles = tile_store[:, 0].reshape(store_span * blocks_here, BLOCK, width)
    value_tiles = tile_store[:, 1].reshape(store_span * blocks_here, BLOCK, width)
    chosen = lax.dynamic_index_in_dim(selected, group_index, 1, keepdims=False)
    live_mask = lax.dynamic_index_in_dim(live_slots, group_index, 1, keepdims=False)
    block_ids = ctx_index * blocks_here + jnp.arange(blocks_here, dtype=jnp.int32)
    local_block = chosen % blocks_here
    per_part = blocks_here // parts_count
    rolled_block = (local_block // per_part - part_index) % parts_count * per_part + local_block % per_part
    offset = jnp.clip(ctx_index - chosen // blocks_here, 0, REACH)
    placed = jnp.where(
        even, jnp.array([0, 1, 5, 2, 6, 3, 7], jnp.int32)[offset], jnp.array([0, 4, 5, 1, 6, 2, 7], jnp.int32)[offset]
    )
    slot_index = placed * blocks_here + rolled_block
    code = jnp.where(live_mask == 1, jnp.where(chosen < block_ids[:, None], 2, 1), 0)
    query_grad, key_grad, value_grad = local_grads(
        queries, out_grad, key_tiles, value_tiles, slot_index, code, inv_root
    )
    grads = jnp.stack([key_grad, value_grad]).reshape(2, store_span, tokens_here, width)
    half = store_span // 2
    back = swap_cores(grads[:, half:].astype(jnp.bfloat16), "ctx").astype(jnp.float32)
    totals = grads[:, :half] + back
    sent = totals.astype(jnp.bfloat16)

    def reduce_parts(lo, hi):
        part = totals[:, lo:hi, :quarter]
        for step in range(1, parts_count):
            piece = sent[:, lo:hi, step * quarter:(step + 1) * quarter]
            part = part + cycled(piece, "sub", step).astype(jnp.float32)
        return part

    reduced = reduce_parts(0, half)
    running = reduced[:, 0]
    for step in range(1, half):
        term = reduced[:, step].astype(jnp.bfloat16)
        running = running + chip_return(term, "ctx", step).astype(jnp.float32)
    mine = running.astype(jnp.bfloat16)
    by_group = jnp.stack([mine] + [cycled(mine, "grp", -step) for step in range(1, groups)])
    by_part = jnp.stack([by_group] + [cycled(by_group, "sub", -step) for step in range(1, parts_count)])
    part_order = (jnp.arange(parts_count) - part_index) % parts_count
    group_order = (jnp.arange(groups) - group_index) % groups
    flat_order = (part_order[None, :] * groups + group_order[:, None]).reshape(-1)
    ordered = jnp.take(by_part.reshape((parts_count * groups,) + mine.shape), flat_order, axis=0)
    ordered = ordered.reshape((groups, parts_count) + mine.shape)
    summed = jnp.transpose(ordered, (2, 0, 1, 3, 4)).reshape(2, groups, tokens_here, width)
    summed = summed.astype(jnp.float32)
    return (query_grad, summed[0], summed[1])


def solution(mesh):
    ctx_count, head_count = mesh.devices.shape
    groups = 4
    split = Mesh(
        np.asarray(mesh.devices).reshape(ctx_count, groups, head_count // groups),
        ("ctx", "grp", "sub"),
    )
    heads = ("grp", "sub")
    return jax.shard_map(
        per_device,
        mesh=split,
        in_specs=(
            P("ctx", heads, None),
            P(None, "ctx", None),
            P(None, "ctx", None),
            P("ctx", heads, None),
            P("ctx", None, None),
            P("ctx", None, None),
        ),
        out_specs=(P("ctx", heads, None), P(None, "ctx", None), P(None, "ctx", None)),
        check_vma=False,
    )
```
